32 devices in a mesh: az: 32 (over z, y, x, core).
Axes of the slice: x: 2, y: 2, z: 4, core: 2. Of those that a mesh axis runs over, the one named last changes fastest.
Arguments:
- source: float32 [128, 2, 256, 256], P('az'), may hold values from -20 to 20
- coupling: float32 [128, 256, 256], P('az'), may hold values from 0.25 to 1
- wavenumber: float32 [128, 256, 256], P('az'), may hold values from 0.5 to 2
- lateral_x: float32 [256, 256], replicated, may hold values from -0.375 to 0.375
- lateral_r: float32 [256, 256], replicated, may hold values from -0.375 to 0.375
Outputs:
- solution: float32 [128, 2, 256, 256], P('az')
- residual: float32 [128, 2, 256, 256], P('az')
- history: float32 [3], replicated
The draws below stay inside these ranges and needn't reach their ends.
All inputs are finite; a program needn't handle non-finite values.
Results may differ from the reference program's by a relative error of at most 0.0001.
Values sent between devices are 32-bit elements; how exact they have to be, the bound alone decides.
No kernel may reach another device: no remote copies, remote signals or barrier semaphores. Data moves between devices by JAX's collectives and lax.ppermute only.
A program may use at most 64 MiB of HBM per device.

```python
import math
import jax
import jax.numpy as jnp
from jax import lax

NX = 256
NR = 256
ITERS = 3
NPHI = 128


def draw_source(key, part):
    plane = jnp.arange(NPHI).astype(jnp.float32) / NPHI
    row_pos = jnp.arange(NX).astype(jnp.float32) / NX
    values = jnp.clip(jax.random.normal(key, (NPHI, 2, NX, NR), jnp.float32), -6.0, 6.0)
    plane_scale = 10.0 ** (0.5 * (plane - 0.5))
    row_scale = 10.0 ** (0.5 * (row_pos - 0.5))
    return values * plane_scale[:, None, None, None] * row_scale[None, None, :, None]


def steps_of(rng, shape, split, low, top_value):
    factor_of, own = 1.0, jax.random.fold_in(rng, 6)
    for axis_at, shards_of in split:
        steps = jnp.exp(jax.random.uniform(jax.random.fold_in(own, axis_at), (shards_of,), jnp.float32, low / len(split), top_value / len(split)))
        factor_of = factor_of * jnp.repeat(steps, shape[axis_at] // shards_of).reshape([-1 if axis == axis_at else 1 for axis in range(len(shape))])
    return factor_of


def bell_draw(key, dims, scale, reach, dtype=jnp.bfloat16):
    entries = jax.random.normal(key, dims, jnp.float32) * scale
    return jnp.minimum(jnp.maximum(entries, -reach), reach).astype(dtype)


def setup_inputs(seed: int = 0) -> dict:
    key_list = jax.random.split(jax.random.key(seed), 6)
    return {
        "source": draw_source(jax.random.fold_in(key_list[5], 71), 0),
        "coupling": jnp.clip(jnp.exp(math.log(1.0) - 1.3862944 * jax.random.uniform(key_list[1], (NPHI, NX, NR), jnp.float32) ** steps_of(key_list[1], (NPHI, NX, NR), ((0, 32),), -0.2, 0.2)), 0.25, 1.0),
        "wavenumber": jnp.clip(jnp.exp(math.log(2.0) - 1.3862944 * jax.random.uniform(key_list[2], (NPHI, NX, NR), jnp.float32) ** steps_of(key_list[2], (NPHI, NX, NR), ((0, 32),), -0.2, 0.2)), 0.5, 2.0),
        "lateral_x": bell_draw(key_list[3], (NX, NX), NX ** -0.5, 0.375, jnp.float32),
        "lateral_r": bell_draw(key_list[4], (NR, NR), NR ** -0.5, 0.375, jnp.float32),
    }


damping = 0.4
epsilon = 1e-06

def sine_basis(count):
    index = jnp.arange(count).astype(jnp.float32) + 1.0
    angle_grid = math.pi / (count + 1) * index[:, None] * index[None, :]
    table = math.sqrt(2.0 / (count + 1)) * jnp.sin(angle_grid)
    spectrum = 2.0 - 2.0 * jnp.cos(math.pi / (count + 1) * index)
    return (table, spectrum)

def transform(field, trans_x, trans_r):
    inner = jnp.einsum('ij,pcjk->pcik', trans_x, field, precision=lax.Precision.HIGHEST)
    return jnp.einsum('pcik,kl->pcil', inner, trans_r, precision=lax.Precision.HIGHEST)

def precondition(field, trans_x, trans_r, inv_real, inv_imag):
    spectral = transform(field, trans_x, trans_r)
    real_part = spectral[:, 0] * inv_real - spectral[:, 1] * inv_imag
    imag_part = spectral[:, 1] * inv_real + spectral[:, 0] * inv_imag
    return transform(jnp.stack([real_part, imag_part], axis=1), trans_x, trans_r)

def lateral(field, lateral_x, lateral_r):
    padded = jnp.pad(field, ((0, 0), (0, 0), (1, 1), (1, 1)))
    stencil = 4.0 * field - padded[:, :, 2:, 1:-1] - padded[:, :, :-2, 1:-1] - padded[:, :, 1:-1, 2:] - padded[:, :, 1:-1, :-2]
    dense = jnp.einsum('ij,pcjk->pcik', lateral_x, field, precision=lax.Precision.HIGHEST)
    dense = dense + jnp.einsum('pcik,kl->pcil', field, lateral_r, precision=lax.Precision.HIGHEST)
    return stencil + dense

def operate(field, before, after, coupling, coupling_prev, wavenumber, lateral_x, lateral_r):
    result = lateral(field, lateral_x, lateral_r) - wavenumber[:, None] * field
    result = result + coupling[:, None] * (field - after) + coupling_prev[:, None] * (field - before)
    return result

def tables(count_x, count_r):
    trans_x, spec_x = sine_basis(count_x)
    trans_r, spec_r = sine_basis(count_r)
    denom_real = spec_x[:, None] + spec_r[None, :]
    magnitude = denom_real * denom_real + 1.0
    return (trans_x, trans_r, denom_real / magnitude, -1.0 / magnitude)

def reference(source, coupling, wavenumber, lateral_x, lateral_r):
    trans_x, trans_r, inv_real, inv_imag = tables(source.shape[2], source.shape[3])
    coupling_prev = jnp.roll(coupling, 1, axis=0)
    solution = jnp.zeros_like(source)
    residual = source
    base = jnp.sum(source * source)
    norms = []
    for iteration in range(ITERS):
        update = precondition(residual, trans_x, trans_r, inv_real, inv_imag)
        before = jnp.roll(update, 1, axis=0)
        after = jnp.roll(update, -1, axis=0)
        solution = solution + damping * update
        residual = residual - damping * operate(update, before, after, coupling, coupling_prev, wavenumber, lateral_x, lateral_r)
        norms.append(jnp.sqrt(jnp.sum(residual * residual) / (base + epsilon)))
    return (solution, residual, jnp.stack(norms))
```

```python
import math

import jax
import jax.numpy as jnp
from jax import lax
from jax.sharding import PartitionSpec as P

ITERS = 3


damping = 0.4
epsilon = 1e-06

PREC = lax.Precision.HIGHEST


def shift_ring(value, axis, steps):
    count = lax.axis_size(axis)
    pairs = [(source, (source + steps) % count) for source in range(count)]
    return lax.ppermute(value, axis, pairs)


def all_sum(value, axis):
    count = lax.axis_size(axis)
    if count & (count - 1):
        return lax.psum(value, axis)
    step = 1
    while step < count:
        pairs = [(i, i ^ step) for i in range(count)]
        value = value + lax.ppermute(value, axis, pairs)
        step *= 2
    return value


def sine_basis(count):
    index = jnp.arange(count).astype(jnp.float32) + 1.0
    angle_grid = math.pi / (count + 1) * index[:, None] * index[None, :]
    table = math.sqrt(2.0 / (count + 1)) * jnp.sin(angle_grid)
    spectrum = 2.0 - 2.0 * jnp.cos(math.pi / (count + 1) * index)
    return (table, spectrum)


def transform(field, trans_x, trans_r):
    inner = jnp.einsum("ij,pcjk->pcik", trans_x, field, precision=PREC)
    return jnp.einsum("pcik,kl->pcil", inner, trans_r, precision=PREC)


def precondition(field, trans_x, trans_r, inv_real, inv_imag):
    spectral = transform(field, trans_x, trans_r)
    real_part = spectral[:, 0] * inv_real - spectral[:, 1] * inv_imag
    imag_part = spectral[:, 1] * inv_real + spectral[:, 0] * inv_imag
    return transform(jnp.stack([real_part, imag_part], axis=1), trans_x, trans_r)


def lateral(field, lateral_x, lateral_r):
    padded = jnp.pad(field, ((0, 0), (0, 0), (1, 1), (1, 1)))
    stencil = (
        4.0 * field
        - padded[:, :, 2:, 1:-1]
        - padded[:, :, :-2, 1:-1]
        - padded[:, :, 1:-1, 2:]
        - padded[:, :, 1:-1, :-2]
    )
    dense = jnp.einsum("ij,pcjk->pcik", lateral_x, field, precision=PREC)
    dense = dense + jnp.einsum("pcik,kl->pcil", field, lateral_r, precision=PREC)
    return stencil + dense


def operate(field, before, after, coupling, coupling_prev, wavenumber, lateral_x, lateral_r):
    result = lateral(field, lateral_x, lateral_r) - wavenumber[:, None] * field
    result = (
        result + coupling[:, None] * (field - after) + coupling_prev[:, None] * (field - before)
    )
    return result


def on_device(source, coupling, wavenumber, lateral_x, lateral_r):
    planes = source.shape[0]
    trans_x, spec_x = sine_basis(source.shape[2])
    trans_r, spec_r = sine_basis(source.shape[3])
    denom_real = spec_x[:, None] + spec_r[None, :]
    magnitude = denom_real * denom_real + 1.0
    inv_real = denom_real / magnitude
    inv_imag = -1.0 / magnitude
    rim = shift_ring(coupling[-1:], "az", 1)
    coupling_prev = jnp.concatenate([rim, coupling[:-1]], axis=0)
    pre = lambda f: precondition(f, trans_x, trans_r, inv_real, inv_imag)
    mid = slice(1, planes - 1)
    split = planes >= 3

    def edges_of(a):
        return jnp.concatenate([a[:1], a[-1:]], axis=0)

    if split:
        res_e, res_i = edges_of(source), source[mid]
        sol_e = jnp.zeros_like(res_e)
        sol_i = jnp.zeros_like(res_i)
        c_e, c_i = edges_of(coupling), coupling[mid]
        cp_e, cp_i = edges_of(coupling_prev), coupling_prev[mid]
        w_e, w_i = edges_of(wavenumber), wavenumber[mid]
    else:
        residual = source
        solution_all = jnp.zeros_like(source)
    local_sums = [jnp.sum(source * source)]
    for iteration in range(ITERS):
        if split:
            upd_e = pre(res_e)
            halo_before = shift_ring(upd_e[1:2], "az", 1)
            halo_after = shift_ring(upd_e[0:1], "az", -1)
            upd_i = pre(res_i)
            full = jnp.concatenate([upd_e[:1], upd_i, upd_e[1:]], axis=0)
            op_i = operate(
                upd_i, full[: planes - 2], full[2:], c_i, cp_i, w_i, lateral_x, lateral_r
            )
            res_i = res_i - damping * op_i
            sol_i = sol_i + damping * upd_i
            before_e = jnp.concatenate([halo_before, full[planes - 2 : planes - 1]], axis=0)
            after_e = jnp.concatenate([full[1:2], halo_after], axis=0)
            op_e = operate(upd_e, before_e, after_e, c_e, cp_e, w_e, lateral_x, lateral_r)
            res_e = res_e - damping * op_e
            sol_e = sol_e + damping * upd_e
            local_sums.append(jnp.sum(res_i * res_i) + jnp.sum(res_e * res_e))
        else:
            update = pre(residual)
            before = jnp.concatenate([shift_ring(update[-1:], "az", 1), update[:-1]], axis=0)
            after = jnp.concatenate([update[1:], shift_ring(update[:1], "az", -1)], axis=0)
            solution_all = solution_all + damping * update
            residual = residual - damping * operate(
                update, before, after, coupling, coupling_prev, wavenumber, lateral_x, lateral_r
            )
            local_sums.append(jnp.sum(residual * residual))
    if split:
        solution_all = jnp.concatenate([sol_e[:1], sol_i, sol_e[1:]], axis=0)
        residual = jnp.concatenate([res_e[:1], res_i, res_e[1:]], axis=0)
    totals = all_sum(jnp.stack(local_sums), "az")
    history = jnp.sqrt(totals[1:] / (totals[0] + epsilon))
    return (solution_all, residual, history)


def solution(mesh):
    return jax.shard_map(
        on_device,
        mesh=mesh,
        in_specs=(P("az", None, None, None), P("az", None, None), P("az", None, None), P(), P()),
        out_specs=(P("az", None, None, None), P("az", None, None, None), P()),
        check_vma=False,
    )
```

```python
import math

import jax
import jax.numpy as jnp
from jax import lax
from jax.sharding import PartitionSpec as P

ITERS = 3


damping = 0.4
epsilon = 1e-06

PREC = lax.Precision.HIGH


def shift_ring(value, axis, steps):
    count = lax.axis_size(axis)
    pairs = [(source, (source + steps) % count) for source in range(count)]
    return lax.ppermute(value, axis, pairs)


def all_sum(value, axis):
    count = lax.axis_size(axis)
    if count & (count - 1):
        return lax.psum(value, axis)
    step = 1
    while step < count:
        pairs = [(i, i ^ step) for i in range(count)]
        value = value + lax.ppermute(value, axis, pairs)
        step *= 2
    return value


def sine_basis(count):
    index = jnp.arange(count).astype(jnp.float32) + 1.0
    angle_grid = math.pi / (count + 1) * index[:, None] * index[None, :]
    table = math.sqrt(2.0 / (count + 1)) * jnp.sin(angle_grid)
    spectrum = 2.0 - 2.0 * jnp.cos(math.pi / (count + 1) * index)
    return (table, spectrum)


def transform(field, trans_x, trans_r):
    inner = jnp.einsum("ij,pcjk->pcik", trans_x, field, precision=PREC)
    return jnp.einsum("pcik,kl->pcil", inner, trans_r, precision=PREC)


def precondition(field, trans_x, trans_r, inv_real, inv_imag):
    spectral = transform(field, trans_x, trans_r)
    real_part = spectral[:, 0] * inv_real - spectral[:, 1] * inv_imag
    imag_part = spectral[:, 1] * inv_real + spectral[:, 0] * inv_imag
    return transform(jnp.stack([real_part, imag_part], axis=1), trans_x, trans_r)


def lateral(field, lateral_x, lateral_r):
    padded = jnp.pad(field, ((0, 0), (0, 0), (1, 1), (1, 1)))
    stencil = (
        4.0 * field
        - padded[:, :, 2:, 1:-1]
        - padded[:, :, :-2, 1:-1]
        - padded[:, :, 1:-1, 2:]
        - padded[:, :, 1:-1, :-2]
    )
    dense = jnp.einsum("ij,pcjk->pcik", lateral_x, field, precision=PREC)
    dense = dense + jnp.einsum("pcik,kl->pcil", field, lateral_r, precision=PREC)
    return stencil + dense


def operate(field, before, after, coupling, coupling_prev, wavenumber, lateral_x, lateral_r):
    result = lateral(field, lateral_x, lateral_r) - wavenumber[:, None] * field
    result = (
        result + coupling[:, None] * (field - after) + coupling_prev[:, None] * (field - before)
    )
    return result


def on_device(source, coupling, wavenumber, lateral_x, lateral_r):
    planes = source.shape[0]
    trans_x, spec_x = sine_basis(source.shape[2])
    trans_r, spec_r = sine_basis(source.shape[3])
    denom_real = spec_x[:, None] + spec_r[None, :]
    magnitude = denom_real * denom_real + 1.0
    inv_real = denom_real / magnitude
    inv_imag = -1.0 / magnitude
    rim = shift_ring(coupling[-1:], "az", 1)
    coupling_prev = jnp.concatenate([rim, coupling[:-1]], axis=0)
    pre = lambda f: precondition(f, trans_x, trans_r, inv_real, inv_imag)
    mid = slice(1, planes - 1)
    split = planes >= 3

    def edges_of(a):
        return jnp.concatenate([a[:1], a[-1:]], axis=0)

    if split:
        res_e, res_i = edges_of(source), source[mid]
        sol_e = jnp.zeros_like(res_e)
        sol_i = jnp.zeros_like(res_i)
        c_e, c_i = edges_of(coupling), coupling[mid]
        cp_e, cp_i = edges_of(coupling_prev), coupling_prev[mid]
        w_e, w_i = edges_of(wavenumber), wavenumber[mid]
    else:
        residual = source
        solution_all = jnp.zeros_like(source)
    local_sums = [jnp.sum(source * source)]
    for iteration in range(ITERS):
        if split:
            upd_e = pre(res_e)
            halo_before = shift_ring(upd_e[1:2], "az", 1)
            halo_after = shift_ring(upd_e[0:1], "az", -1)
            upd_i = pre(res_i)
            full = jnp.concatenate([upd_e[:1], upd_i, upd_e[1:]], axis=0)
            op_i = operate(
                upd_i, full[: planes - 2], full[2:], c_i, cp_i, w_i, lateral_x, lateral_r
            )
            res_i = res_i - damping * op_i
            sol_i = sol_i + damping * upd_i
            before_e = jnp.concatenate([halo_before, full[planes - 2 : planes - 1]], axis=0)
            after_e = jnp.concatenate([full[1:2], halo_after], axis=0)
            op_e = operate(upd_e, before_e, after_e, c_e, cp_e, w_e, lateral_x, lateral_r)
            res_e = res_e - damping * op_e
            sol_e = sol_e + damping * upd_e
            local_sums.append(jnp.sum(res_i * res_i) + jnp.sum(res_e * res_e))
        else:
            update = pre(residual)
            before = jnp.concatenate([shift_ring(update[-1:], "az", 1), update[:-1]], axis=0)
            after = jnp.concatenate([update[1:], shift_ring(update[:1], "az", -1)], axis=0)
            solution_all = solution_all + damping * update
            residual = residual - damping * operate(
                update, before, after, coupling, coupling_prev, wavenumber, lateral_x, lateral_r
            )
            local_sums.append(jnp.sum(residual * residual))
    if split:
        solution_all = jnp.concatenate([sol_e[:1], sol_i, sol_e[1:]], axis=0)
        residual = jnp.concatenate([res_e[:1], res_i, res_e[1:]], axis=0)
    totals = all_sum(jnp.stack(local_sums), "az")
    history = jnp.sqrt(totals[1:] / (totals[0] + epsilon))
    return (solution_all, residual, history)


def solution(mesh):
    return jax.shard_map(
        on_device,
        mesh=mesh,
        in_specs=(P("az", None, None, None), P("az", None, None), P("az", None, None), P(), P()),
        out_specs=(P("az", None, None, None), P("az", None, None, None), P()),
        check_vma=False,
    )
```

```python
import math

import jax
import jax.numpy as jnp
from jax import lax
from jax.sharding import PartitionSpec as P

ITERS = 3


damping = 0.4
epsilon = 1e-06

PREC = lax.Precision.HIGHEST
PREC_FWD = (PREC, PREC)
PREC_INV = (PREC, PREC)
PREC_LAT = (lax.Precision.HIGH, lax.Precision.HIGH)


def shift_ring(value, axis, steps):
    count = lax.axis_size(axis)
    pairs = [(source, (source + steps) % count) for source in range(count)]
    return lax.ppermute(value, axis, pairs)


def all_sum(value, axis):
    count = lax.axis_size(axis)
    spread = jnp.broadcast_to(value, (count,) + value.shape)
    gathered = lax.all_to_all(spread, axis, 0, 0, tiled=True)
    total = gathered[0]
    for index in range(1, count):
        total = total + gathered[index]
    return total


def sine_basis(count):
    index = jnp.arange(count).astype(jnp.float32) + 1.0
    angle_grid = math.pi / (count + 1) * index[:, None] * index[None, :]
    table = math.sqrt(2.0 / (count + 1)) * jnp.sin(angle_grid)
    spectrum = 2.0 - 2.0 * jnp.cos(math.pi / (count + 1) * index)
    return (table, spectrum)


def transform(field, trans_x, trans_r, precs):
    inner = jnp.einsum("ij,pcjk->pcik", trans_x, field, precision=precs[0])
    return jnp.einsum("pcik,kl->pcil", inner, trans_r, precision=precs[1])


def precondition(field, trans_x, trans_r, inv_real, inv_imag):
    spectral = transform(field, trans_x, trans_r, PREC_FWD)
    real_part = spectral[:, 0] * inv_real - spectral[:, 1] * inv_imag
    imag_part = spectral[:, 1] * inv_real + spectral[:, 0] * inv_imag
    return transform(jnp.stack([real_part, imag_part], axis=1), trans_x, trans_r, PREC_INV)


def lateral(field, lateral_x, lateral_r):
    padded = jnp.pad(field, ((0, 0), (0, 0), (1, 1), (1, 1)))
    stencil = (
        4.0 * field
        - padded[:, :, 2:, 1:-1]
        - padded[:, :, :-2, 1:-1]
        - padded[:, :, 1:-1, 2:]
        - padded[:, :, 1:-1, :-2]
    )
    dense = jnp.einsum("ij,pcjk->pcik", lateral_x, field, precision=PREC_LAT[0])
    dense = dense + jnp.einsum("pcik,kl->pcil", field, lateral_r, precision=PREC_LAT[1])
    return stencil + dense


def operate(field, before, after, coupling, coupling_prev, wavenumber, lateral_x, lateral_r):
    result = lateral(field, lateral_x, lateral_r) - wavenumber[:, None] * field
    result = (
        result + coupling[:, None] * (field - after) + coupling_prev[:, None] * (field - before)
    )
    return result


def on_device(source, coupling, wavenumber, lateral_x, lateral_r):
    planes = source.shape[0]
    trans_x, spec_x = sine_basis(source.shape[2])
    trans_r, spec_r = sine_basis(source.shape[3])
    denom_real = spec_x[:, None] + spec_r[None, :]
    magnitude = denom_real * denom_real + 1.0
    inv_real = denom_real / magnitude
    inv_imag = -1.0 / magnitude
    rim = shift_ring(coupling[-1:], "az", 1)
    coupling_prev = jnp.concatenate([rim, coupling[:-1]], axis=0)
    pre = lambda f: precondition(f, trans_x, trans_r, inv_real, inv_imag)
    mid = slice(1, planes - 1)
    split = planes >= 3

    def edges_of(a):
        return jnp.concatenate([a[:1], a[-1:]], axis=0)

    if split:
        res_e, res_i = edges_of(source), source[mid]
        sol_e = jnp.zeros_like(res_e)
        sol_i = jnp.zeros_like(res_i)
        c_e, c_i = edges_of(coupling), coupling[mid]
        cp_e, cp_i = edges_of(coupling_prev), coupling_prev[mid]
        w_e, w_i = edges_of(wavenumber), wavenumber[mid]
    else:
        residual = source
        solution_all = jnp.zeros_like(source)
    local_sums = [jnp.sum(source * source)]
    for iteration in range(ITERS):
        if split:
            upd_e = pre(res_e)
            halo_before = shift_ring(upd_e[1:2], "az", 1)
            halo_after = shift_ring(upd_e[0:1], "az", -1)
            upd_i = pre(res_i)
            full = jnp.concatenate([upd_e[:1], upd_i, upd_e[1:]], axis=0)
            op_i = operate(
                upd_i, full[: planes - 2], full[2:], c_i, cp_i, w_i, lateral_x, lateral_r
            )
            res_i = res_i - damping * op_i
            sol_i = sol_i + damping * upd_i
            before_e = jnp.concatenate([halo_before, full[planes - 2 : planes - 1]], axis=0)
            after_e = jnp.concatenate([full[1:2], halo_after], axis=0)
            op_e = operate(upd_e, before_e, after_e, c_e, cp_e, w_e, lateral_x, lateral_r)
            res_e = res_e - damping * op_e
            sol_e = sol_e + damping * upd_e
            local_sums.append(jnp.sum(res_i * res_i) + jnp.sum(res_e * res_e))
        else:
            update = pre(residual)
            before = jnp.concatenate([shift_ring(update[-1:], "az", 1), update[:-1]], axis=0)
            after = jnp.concatenate([update[1:], shift_ring(update[:1], "az", -1)], axis=0)
            solution_all = solution_all + damping * update
            residual = residual - damping * operate(
                update, before, after, coupling, coupling_prev, wavenumber, lateral_x, lateral_r
            )
            local_sums.append(jnp.sum(residual * residual))
    if split:
        solution_all = jnp.concatenate([sol_e[:1], sol_i, sol_e[1:]], axis=0)
        residual = jnp.concatenate([res_e[:1], res_i, res_e[1:]], axis=0)
    totals = all_sum(jnp.stack(local_sums), "az")
    history = jnp.sqrt(totals[1:] / (totals[0] + epsilon))
    return (solution_all, residual, history)


def solution(mesh):
    return jax.shard_map(
        on_device,
        mesh=mesh,
        in_specs=(P("az", None, None, None), P("az", None, None), P("az", None, None), P(), P()),
        out_specs=(P("az", None, None, None), P("az", None, None, None), P()),
        check_vma=False,
    )
```

```python
import math

import jax
import jax.numpy as jnp
from jax import lax
from jax.experimental import pallas as pl
from jax.sharding import PartitionSpec as P

ITERS = 3


damping = 0.4
epsilon = 1e-06

def shift_ring(value, axis, steps):
    count = lax.axis_size(axis)
    pairs = [(source, (source + steps) % count) for source in range(count)]
    return lax.ppermute(value, axis, pairs)


def all_sum(value, axis):
    count = lax.axis_size(axis)
    spread = jnp.broadcast_to(value, (count,) + value.shape)
    gathered = lax.all_to_all(spread, axis, 0, 0, tiled=True)
    total = gathered[0]
    for index in range(1, count):
        total = total + gathered[index]
    return total


def split_bf16(a):
    high = a.astype(jnp.bfloat16)
    low = (a - high.astype(jnp.float32)).astype(jnp.bfloat16)
    return high, low


def split_table(a):
    high = lax.reduce_precision(a, exponent_bits=8, mantissa_bits=7)
    return high.astype(jnp.bfloat16), (a - high).astype(jnp.bfloat16)


def plane_kernel(qx_ref, qr_ref, ir_ref, ii_ref, lxh_ref, lxl_ref, lrh_ref, lrl_ref, f_ref, u_ref, lat_ref):
    def dot(a, b):
        return jnp.dot(a, b, precision=lax.Precision.HIGHEST, preferred_element_type=jnp.float32)

    def bdot(a, b):
        return jnp.dot(a, b, preferred_element_type=jnp.float32)

    qx = qx_ref[...]
    qr = qr_ref[...]
    s0 = dot(dot(qx, f_ref[0, 0]), qr)
    s1 = dot(dot(qx, f_ref[0, 1]), qr)
    inv_real = ir_ref[...]
    inv_imag = ii_ref[...]
    spectral = (s0 * inv_real - s1 * inv_imag, s1 * inv_real + s0 * inv_imag)
    lxh, lxl = lxh_ref[...], lxl_ref[...]
    lrh, lrl = lrh_ref[...], lrl_ref[...]
    for part in range(2):
        u = dot(dot(qx, spectral[part]), qr)
        u_ref[0, part] = u
        uh, ul = split_bf16(u)
        along_x = bdot(lxh, uh) + bdot(lxh, ul) + bdot(lxl, uh)
        along_r = bdot(uh, lrh) + bdot(ul, lrh) + bdot(uh, lrl)
        lat_ref[0, part] = along_x + along_r


def plane_step(field, tabs):
    count = field.shape[0]
    nx, nr = field.shape[2], field.shape[3]
    specs = [
        pl.BlockSpec(t.shape, lambda p: (0, 0)) for t in tabs
    ]
    block = pl.BlockSpec((1, 2, nx, nr), lambda p: (p, 0, 0, 0))
    shape = jax.ShapeDtypeStruct(field.shape, jnp.float32)
    return pl.pallas_call(
        plane_kernel,
        grid=(count,),
        in_specs=specs + [block],
        out_specs=[block, block],
        out_shape=[shape, shape],
    )(*tabs, field)


def sine_basis(count):
    index = jnp.arange(count).astype(jnp.float32) + 1.0
    angle_grid = math.pi / (count + 1) * index[:, None] * index[None, :]
    table = math.sqrt(2.0 / (count + 1)) * jnp.sin(angle_grid)
    spectrum = 2.0 - 2.0 * jnp.cos(math.pi / (count + 1) * index)
    return (table, spectrum)


def stencil_of(field):
    padded = jnp.pad(field, ((0, 0), (0, 0), (1, 1), (1, 1)))
    return (
        4.0 * field
        - padded[:, :, 2:, 1:-1]
        - padded[:, :, :-2, 1:-1]
        - padded[:, :, 1:-1, 2:]
        - padded[:, :, 1:-1, :-2]
    )


def operate(field, dense, before, after, coupling, coupling_prev, wavenumber):
    result = (stencil_of(field) + dense) - wavenumber[:, None] * field
    result = (
        result + coupling[:, None] * (field - after) + coupling_prev[:, None] * (field - before)
    )
    return result


def on_device(source, coupling, wavenumber, lateral_x, lateral_r):
    planes = source.shape[0]
    trans_x, spec_x = sine_basis(source.shape[2])
    trans_r, spec_r = sine_basis(source.shape[3])
    denom_real = spec_x[:, None] + spec_r[None, :]
    magnitude = denom_real * denom_real + 1.0
    inv_real = denom_real / magnitude
    inv_imag = -1.0 / magnitude
    tabs = (trans_x, trans_r, inv_real, inv_imag) + split_table(lateral_x) + split_table(lateral_r)
    rim = shift_ring(coupling[-1:], "az", 1)
    coupling_prev = jnp.concatenate([rim, coupling[:-1]], axis=0)
    mid = slice(1, planes - 1)
    split = planes >= 3

    def edges_of(a):
        return jnp.concatenate([a[:1], a[-1:]], axis=0)

    if split:
        res_e, res_i = edges_of(source), source[mid]
        sol_e = jnp.zeros_like(res_e)
        sol_i = jnp.zeros_like(res_i)
        c_e, c_i = edges_of(coupling), coupling[mid]
        cp_e, cp_i = edges_of(coupling_prev), coupling_prev[mid]
        w_e, w_i = edges_of(wavenumber), wavenumber[mid]
    else:
        residual = source
        solution_all = jnp.zeros_like(source)
    local_sums = [jnp.sum(source * source)]
    for iteration in range(ITERS):
        if split:
            upd_e, lat_e = plane_step(res_e, tabs)
            halo_before = shift_ring(upd_e[1:2], "az", 1)
            halo_after = shift_ring(upd_e[0:1], "az", -1)
            upd_i, lat_i = plane_step(res_i, tabs)
            full = jnp.concatenate([upd_e[:1], upd_i, upd_e[1:]], axis=0)
            op_i = operate(upd_i, lat_i, full[: planes - 2], full[2:], c_i, cp_i, w_i)
            res_i = res_i - damping * op_i
            sol_i = sol_i + damping * upd_i
            before_e = jnp.concatenate([halo_before, full[planes - 2 : planes - 1]], axis=0)
            after_e = jnp.concatenate([full[1:2], halo_after], axis=0)
            op_e = operate(upd_e, lat_e, before_e, after_e, c_e, cp_e, w_e)
            res_e = res_e - damping * op_e
            sol_e = sol_e + damping * upd_e
            local_sums.append(jnp.sum(res_i * res_i) + jnp.sum(res_e * res_e))
        else:
            update, lat = plane_step(residual, tabs)
            before = jnp.concatenate([shift_ring(update[-1:], "az", 1), update[:-1]], axis=0)
            after = jnp.concatenate([update[1:], shift_ring(update[:1], "az", -1)], axis=0)
            solution_all = solution_all + damping * update
            residual = residual - damping * operate(
                update, lat, before, after, coupling, coupling_prev, wavenumber
            )
            local_sums.append(jnp.sum(residual * residual))
    if split:
        solution_all = jnp.concatenate([sol_e[:1], sol_i, sol_e[1:]], axis=0)
        residual = jnp.concatenate([res_e[:1], res_i, res_e[1:]], axis=0)
    totals = all_sum(jnp.stack(local_sums), "az")
    history = jnp.sqrt(totals[1:] / (totals[0] + epsilon))
    return (solution_all, residual, history)


def solution(mesh):
    return jax.shard_map(
        on_device,
        mesh=mesh,
        in_specs=(P("az", None, None, None), P("az", None, None), P("az", None, None), P(), P()),
        out_specs=(P("az", None, None, None), P("az", None, None, None), P()),
        check_vma=False,
    )
```

```python
import math

import jax
import jax.numpy as jnp
from jax import lax
from jax.sharding import PartitionSpec as P

ITERS = 3


damping = 0.4
epsilon = 1e-06

PREC = lax.Precision.HIGHEST
PREC_FWD = (PREC, PREC)
PREC_INV = (PREC, PREC)
PREC_LAT = (lax.Precision.HIGH, lax.Precision.HIGH)


def shift_ring(value, axis, steps):
    count = lax.axis_size(axis)
    pairs = [(source, (source + steps) % count) for source in range(count)]
    return lax.ppermute(value, axis, pairs)


def all_sum(value, axis):
    count = lax.axis_size(axis)
    spread = jnp.broadcast_to(value, (count,) + value.shape)
    gathered = lax.all_to_all(spread, axis, 0, 0, tiled=True)
    total = gathered[0]
    for index in range(1, count):
        total = total + gathered[index]
    return total


def sine_basis(count):
    index = jnp.arange(count).astype(jnp.float32) + 1.0
    angle_grid = math.pi / (count + 1) * index[:, None] * index[None, :]
    table = math.sqrt(2.0 / (count + 1)) * jnp.sin(angle_grid)
    spectrum = 2.0 - 2.0 * jnp.cos(math.pi / (count + 1) * index)
    return (table, spectrum)


def transform(field, trans_x, trans_r, precs):
    inner = jnp.einsum("ij,pcjk->pcik", trans_x, field, precision=precs[0])
    return jnp.einsum("pcik,kl->pcil", inner, trans_r, precision=precs[1])


def forward(field, trans_x, trans_r, inv_real, inv_imag):
    spectral = transform(field, trans_x, trans_r, PREC_FWD)
    real_part = spectral[:, 0] * inv_real - spectral[:, 1] * inv_imag
    imag_part = spectral[:, 1] * inv_real + spectral[:, 0] * inv_imag
    return jnp.stack([real_part, imag_part], axis=1)


def precondition(field, trans_x, trans_r, inv_real, inv_imag):
    scaled = forward(field, trans_x, trans_r, inv_real, inv_imag)
    return transform(scaled, trans_x, trans_r, PREC_INV)


def lateral(field, lateral_x, lateral_r):
    padded = jnp.pad(field, ((0, 0), (0, 0), (1, 1), (1, 1)))
    stencil = (
        4.0 * field
        - padded[:, :, 2:, 1:-1]
        - padded[:, :, :-2, 1:-1]
        - padded[:, :, 1:-1, 2:]
        - padded[:, :, 1:-1, :-2]
    )
    dense = jnp.einsum("ij,pcjk->pcik", lateral_x, field, precision=PREC_LAT[0])
    dense = dense + jnp.einsum("pcik,kl->pcil", field, lateral_r, precision=PREC_LAT[1])
    return stencil + dense


def operate(field, before, after, coupling, coupling_prev, wavenumber, lateral_x, lateral_r):
    result = lateral(field, lateral_x, lateral_r) - wavenumber[:, None] * field
    result = (
        result + coupling[:, None] * (field - after) + coupling_prev[:, None] * (field - before)
    )
    return result


def on_device(source, coupling, wavenumber, lateral_x, lateral_r):
    planes = source.shape[0]
    trans_x, spec_x = sine_basis(source.shape[2])
    trans_r, spec_r = sine_basis(source.shape[3])
    denom_real = spec_x[:, None] + spec_r[None, :]
    magnitude = denom_real * denom_real + 1.0
    inv_real = denom_real / magnitude
    inv_imag = -1.0 / magnitude
    rim = shift_ring(coupling[-1:], "az", 1)
    coupling_prev = jnp.concatenate([rim, coupling[:-1]], axis=0)
    pre = lambda f: precondition(f, trans_x, trans_r, inv_real, inv_imag)
    mid = slice(1, planes - 1)
    split = planes >= 3

    def edges_of(a):
        return jnp.concatenate([a[:1], a[-1:]], axis=0)

    if split:
        residual = source
        sol_e = jnp.zeros_like(edges_of(source))
        sol_i = jnp.zeros_like(source[mid])
        c_e, c_i = edges_of(coupling), coupling[mid]
        cp_e, cp_i = edges_of(coupling_prev), coupling_prev[mid]
        w_e, w_i = edges_of(wavenumber), wavenumber[mid]
    else:
        residual = source
        solution_all = jnp.zeros_like(source)
    local_sums = [jnp.sum(source * source)]
    for iteration in range(ITERS):
        if split:
            scaled = forward(residual, trans_x, trans_r, inv_real, inv_imag)
            upd_e = transform(edges_of(scaled), trans_x, trans_r, PREC_INV)
            halo_before = shift_ring(upd_e[1:2], "az", 1)
            halo_after = shift_ring(upd_e[0:1], "az", -1)
            upd_i = transform(scaled[mid], trans_x, trans_r, PREC_INV)
            res_i = residual[mid]
            res_e = edges_of(residual)
            full = jnp.concatenate([upd_e[:1], upd_i, upd_e[1:]], axis=0)
            op_i = operate(
                upd_i, full[: planes - 2], full[2:], c_i, cp_i, w_i, lateral_x, lateral_r
            )
            res_i = res_i - damping * op_i
            sol_i = sol_i + damping * upd_i
            before_e = jnp.concatenate([halo_before, full[planes - 2 : planes - 1]], axis=0)
            after_e = jnp.concatenate([full[1:2], halo_after], axis=0)
            op_e = operate(upd_e, before_e, after_e, c_e, cp_e, w_e, lateral_x, lateral_r)
            res_e = res_e - damping * op_e
            sol_e = sol_e + damping * upd_e
            local_sums.append(jnp.sum(res_i * res_i) + jnp.sum(res_e * res_e))
            residual = jnp.concatenate([res_e[:1], res_i, res_e[1:]], axis=0)
        else:
            update = pre(residual)
            before = jnp.concatenate([shift_ring(update[-1:], "az", 1), update[:-1]], axis=0)
            after = jnp.concatenate([update[1:], shift_ring(update[:1], "az", -1)], axis=0)
            solution_all = solution_all + damping * update
            residual = residual - damping * operate(
                update, before, after, coupling, coupling_prev, wavenumber, lateral_x, lateral_r
            )
            local_sums.append(jnp.sum(residual * residual))
    if split:
        solution_all = jnp.concatenate([sol_e[:1], sol_i, sol_e[1:]], axis=0)
    totals = all_sum(jnp.stack(local_sums), "az")
    history = jnp.sqrt(totals[1:] / (totals[0] + epsilon))
    return (solution_all, residual, history)


def solution(mesh):
    return jax.shard_map(
        on_device,
        mesh=mesh,
        in_specs=(P("az", None, None, None), P("az", None, None), P("az", None, None), P(), P()),
        out_specs=(P("az", None, None, None), P("az", None, None, None), P()),
        check_vma=False,
    )
```

```python
import math

import jax
import jax.numpy as jnp
from jax import lax
from jax.sharding import PartitionSpec as P

ITERS = 3


damping = 0.4
epsilon = 1e-06

PREC = lax.Precision.HIGHEST
PREC_FWD = (PREC, PREC)
PREC_INV = (PREC, PREC)
PREC_LAT = (lax.Precision.HIGH, lax.Precision.HIGH)


def shift_ring(value, axis, steps):
    count = lax.axis_size(axis)
    pairs = [(source, (source + steps) % count) for source in range(count)]
    return lax.ppermute(value, axis, pairs)


def all_sum(value, axis):
    count = lax.axis_size(axis)
    spread = jnp.broadcast_to(value, (count,) + value.shape)
    gathered = lax.all_to_all(spread, axis, 0, 0, tiled=True)
    total = gathered[0]
    for index in range(1, count):
        total = total + gathered[index]
    return total


def sine_basis(count):
    index = jnp.arange(count).astype(jnp.float32) + 1.0
    angle_grid = math.pi / (count + 1) * index[:, None] * index[None, :]
    table = math.sqrt(2.0 / (count + 1)) * jnp.sin(angle_grid)
    spectrum = 2.0 - 2.0 * jnp.cos(math.pi / (count + 1) * index)
    return (table, spectrum)


def transform(field, trans_x, trans_r, precs):
    inner = jnp.einsum("ij,pcjk->pcik", trans_x, field, precision=precs[0])
    return jnp.einsum("pcik,kl->pcil", inner, trans_r, precision=precs[1])


def forward(field, trans_x, trans_r, inv_real, inv_imag):
    spectral = transform(field, trans_x, trans_r, PREC_FWD)
    real_part = spectral[:, 0] * inv_real - spectral[:, 1] * inv_imag
    imag_part = spectral[:, 1] * inv_real + spectral[:, 0] * inv_imag
    return jnp.stack([real_part, imag_part], axis=1)


def precondition(field, trans_x, trans_r, inv_real, inv_imag):
    scaled = forward(field, trans_x, trans_r, inv_real, inv_imag)
    return transform(scaled, trans_x, trans_r, PREC_INV)


def lateral(field, previous, lateral_x, lateral_r):
    shifted = jnp.stack(
        [previous[:, 0] + field[:, 1], previous[:, 1] - field[:, 0]], axis=1
    )
    dense = jnp.einsum("ij,pcjk->pcik", lateral_x, field, precision=PREC_LAT[0])
    dense = dense + jnp.einsum("pcik,kl->pcil", field, lateral_r, precision=PREC_LAT[1])
    return shifted + dense


def operate(field, previous, before, after, coupling, coupling_prev, wavenumber, lateral_x, lateral_r):
    result = lateral(field, previous, lateral_x, lateral_r) - wavenumber[:, None] * field
    result = (
        result + coupling[:, None] * (field - after) + coupling_prev[:, None] * (field - before)
    )
    return result


def on_device(source, coupling, wavenumber, lateral_x, lateral_r):
    planes = source.shape[0]
    trans_x, spec_x = sine_basis(source.shape[2])
    trans_r, spec_r = sine_basis(source.shape[3])
    denom_real = spec_x[:, None] + spec_r[None, :]
    magnitude = denom_real * denom_real + 1.0
    inv_real = denom_real / magnitude
    inv_imag = -1.0 / magnitude
    rim = shift_ring(coupling[-1:], "az", 1)
    coupling_prev = jnp.concatenate([rim, coupling[:-1]], axis=0)
    pre = lambda f: precondition(f, trans_x, trans_r, inv_real, inv_imag)
    mid = slice(1, planes - 1)
    split = planes >= 3

    def edges_of(a):
        return jnp.concatenate([a[:1], a[-1:]], axis=0)

    if split:
        residual = source
        sol_e = jnp.zeros_like(edges_of(source))
        sol_i = jnp.zeros_like(source[mid])
        c_e, c_i = edges_of(coupling), coupling[mid]
        cp_e, cp_i = edges_of(coupling_prev), coupling_prev[mid]
        w_e, w_i = edges_of(wavenumber), wavenumber[mid]
    else:
        residual = source
        solution_all = jnp.zeros_like(source)
    local_sums = [jnp.sum(source * source)]
    for iteration in range(ITERS):
        if split:
            scaled = forward(residual, trans_x, trans_r, inv_real, inv_imag)
            upd_e = transform(edges_of(scaled), trans_x, trans_r, PREC_INV)
            halo_before = shift_ring(upd_e[1:2], "az", 1)
            halo_after = shift_ring(upd_e[0:1], "az", -1)
            upd_i = transform(scaled[mid], trans_x, trans_r, PREC_INV)
            res_i = residual[mid]
            res_e = edges_of(residual)
            full = jnp.concatenate([upd_e[:1], upd_i, upd_e[1:]], axis=0)
            op_i = operate(
                upd_i, res_i, full[: planes - 2], full[2:], c_i, cp_i, w_i, lateral_x, lateral_r
            )
            res_i = res_i - damping * op_i
            sol_i = sol_i + damping * upd_i
            before_e = jnp.concatenate([halo_before, full[planes - 2 : planes - 1]], axis=0)
            after_e = jnp.concatenate([full[1:2], halo_after], axis=0)
            op_e = operate(
                upd_e, res_e, before_e, after_e, c_e, cp_e, w_e, lateral_x, lateral_r
            )
            res_e = res_e - damping * op_e
            sol_e = sol_e + damping * upd_e
            local_sums.append(jnp.sum(res_i * res_i) + jnp.sum(res_e * res_e))
            residual = jnp.concatenate([res_e[:1], res_i, res_e[1:]], axis=0)
        else:
            update = pre(residual)
            before = jnp.concatenate([shift_ring(update[-1:], "az", 1), update[:-1]], axis=0)
            after = jnp.concatenate([update[1:], shift_ring(update[:1], "az", -1)], axis=0)
            solution_all = solution_all + damping * update
            residual = residual - damping * operate(
                update, residual, before, after, coupling, coupling_prev, wavenumber,
                lateral_x, lateral_r,
            )
            local_sums.append(jnp.sum(residual * residual))
    if split:
        solution_all = jnp.concatenate([sol_e[:1], sol_i, sol_e[1:]], axis=0)
    totals = all_sum(jnp.stack(local_sums), "az")
    history = jnp.sqrt(totals[1:] / (totals[0] + epsilon))
    return (solution_all, residual, history)


def solution(mesh):
    return jax.shard_map(
        on_device,
        mesh=mesh,
        in_specs=(P("az", None, None, None), P("az", None, None), P("az", None, None), P(), P()),
        out_specs=(P("az", None, None, None), P("az", None, None, None), P()),
        check_vma=False,
    )
```

```python
import math

import jax
import jax.numpy as jnp
from jax import lax
from jax.sharding import PartitionSpec as P

ITERS = 3


damping = 0.4
epsilon = 1e-06

PREC = lax.Precision.HIGHEST
PREC_FWD = (PREC, PREC)
PREC_INV = (PREC, PREC)
PREC_LAT = (lax.Precision.HIGH, lax.Precision.HIGH)


def shift_ring(value, axis, steps):
    count = lax.axis_size(axis)
    pairs = [(source, (source + steps) % count) for source in range(count)]
    return lax.ppermute(value, axis, pairs)


def all_sum(value, axis):
    count = lax.axis_size(axis)
    spread = jnp.broadcast_to(value, (count,) + value.shape)
    gathered = lax.all_to_all(spread, axis, 0, 0, tiled=True)
    total = gathered[0]
    for index in range(1, count):
        total = total + gathered[index]
    return total


def sine_basis(count):
    index = jnp.arange(count).astype(jnp.float32) + 1.0
    angle_grid = math.pi / (count + 1) * index[:, None] * index[None, :]
    table = math.sqrt(2.0 / (count + 1)) * jnp.sin(angle_grid)
    spectrum = 2.0 - 2.0 * jnp.cos(math.pi / (count + 1) * index)
    return (table, spectrum)


def transform(field, trans_x, trans_r, precs):
    inner = jnp.einsum("ij,pcjk->pcik", trans_x, field, precision=precs[0])
    return jnp.einsum("pcik,kl->pcil", inner, trans_r, precision=precs[1])


def forward(field, trans_x, trans_r, inv_real, inv_imag):
    spectral = transform(field, trans_x, trans_r, PREC_FWD)
    real_part = spectral[:, 0] * inv_real - spectral[:, 1] * inv_imag
    imag_part = spectral[:, 1] * inv_real + spectral[:, 0] * inv_imag
    return jnp.stack([real_part, imag_part], axis=1)


def precondition(field, trans_x, trans_r, inv_real, inv_imag):
    scaled = forward(field, trans_x, trans_r, inv_real, inv_imag)
    return transform(scaled, trans_x, trans_r, PREC_INV)


def lateral(field, lateral_x, lateral_r):
    padded = jnp.pad(field, ((0, 0), (0, 0), (1, 1), (1, 1)))
    stencil = (
        4.0 * field
        - padded[:, :, 2:, 1:-1]
        - padded[:, :, :-2, 1:-1]
        - padded[:, :, 1:-1, 2:]
        - padded[:, :, 1:-1, :-2]
    )
    dense = jnp.einsum("ij,pcjk->pcik", lateral_x, field, precision=PREC_LAT[0])
    dense = dense + jnp.einsum("pcik,kl->pcil", field, lateral_r, precision=PREC_LAT[1])
    return stencil + dense


def operate(field, before, after, coupling, coupling_prev, wavenumber, lateral_x, lateral_r):
    result = lateral(field, lateral_x, lateral_r) - wavenumber[:, None] * field
    result = (
        result + coupling[:, None] * (field - after) + coupling_prev[:, None] * (field - before)
    )
    return result


def on_device(source, coupling, wavenumber, lateral_x, lateral_r):
    planes = source.shape[0]
    trans_x, spec_x = sine_basis(source.shape[2])
    trans_r, spec_r = sine_basis(source.shape[3])
    denom_real = spec_x[:, None] + spec_r[None, :]
    magnitude = denom_real * denom_real + 1.0
    inv_real = denom_real / magnitude
    inv_imag = -1.0 / magnitude
    rim = shift_ring(coupling[-1:], "az", 1)
    coupling_prev = jnp.concatenate([rim, coupling[:-1]], axis=0)
    pre = lambda f: precondition(f, trans_x, trans_r, inv_real, inv_imag)
    mid = slice(1, planes - 1)
    split = planes >= 3

    def edges_of(a):
        return jnp.concatenate([a[:1], a[-1:]], axis=0)

    if split:
        residual = source
        sol_e = jnp.zeros_like(edges_of(source))
        sol_i = jnp.zeros_like(source[mid])
        c_e, c_i = edges_of(coupling), coupling[mid]
        cp_e, cp_i = edges_of(coupling_prev), coupling_prev[mid]
        w_e, w_i = edges_of(wavenumber), wavenumber[mid]
    else:
        residual = source
        solution_all = jnp.zeros_like(source)
    local_sums = [jnp.sum(source * source)]
    for iteration in range(ITERS):
        if split:
            scaled = forward(residual, trans_x, trans_r, inv_real, inv_imag)
            upd_e = transform(edges_of(scaled), trans_x, trans_r, PREC_INV)
            halo_before = shift_ring(upd_e[1:2], "az", 1)
            halo_after = shift_ring(upd_e[0:1], "az", -1)
            upd_i = transform(scaled[mid], trans_x, trans_r, PREC_INV)
            res_i = residual[mid]
            res_e = edges_of(residual)
            full = jnp.concatenate([upd_e[:1], upd_i, upd_e[1:]], axis=0)
            op_i = operate(
                upd_i, full[: planes - 2], full[2:], c_i, cp_i, w_i, lateral_x, lateral_r
            )
            res_i = res_i - damping * op_i
            sol_i = sol_i + damping * upd_i
            before_e = jnp.concatenate([halo_before, full[planes - 2 : planes - 1]], axis=0)
            after_e = jnp.concatenate([full[1:2], halo_after], axis=0)
            op_e = operate(upd_e, before_e, after_e, c_e, cp_e, w_e, lateral_x, lateral_r)
            res_e = res_e - damping * op_e
            sol_e = sol_e + damping * upd_e
            local_sums.append(jnp.sum(res_i * res_i) + jnp.sum(res_e * res_e))
            residual = residual.at[mid].set(res_i)
            residual = residual.at[:1].set(res_e[:1])
            residual = residual.at[planes - 1 :].set(res_e[1:])
        else:
            update = pre(residual)
            before = jnp.concatenate([shift_ring(update[-1:], "az", 1), update[:-1]], axis=0)
            after = jnp.concatenate([update[1:], shift_ring(update[:1], "az", -1)], axis=0)
            solution_all = solution_all + damping * update
            residual = residual - damping * operate(
                update, before, after, coupling, coupling_prev, wavenumber, lateral_x, lateral_r
            )
            local_sums.append(jnp.sum(residual * residual))
    if split:
        solution_all = jnp.concatenate([sol_e[:1], sol_i, sol_e[1:]], axis=0)
    totals = all_sum(jnp.stack(local_sums), "az")
    history = jnp.sqrt(totals[1:] / (totals[0] + epsilon))
    return (solution_all, residual, history)


def solution(mesh):
    return jax.shard_map(
        on_device,
        mesh=mesh,
        in_specs=(P("az", None, None, None), P("az", None, None), P("az", None, None), P(), P()),
        out_specs=(P("az", None, None, None), P("az", None, None, None), P()),
        check_vma=False,
    )
```

```python
import math

import jax
import jax.numpy as jnp
from jax import lax
from jax.sharding import PartitionSpec as P

ITERS = 3


damping = 0.4
epsilon = 1e-06

PREC = lax.Precision.HIGHEST
PREC_FWD = (PREC, PREC)
PREC_INV = (PREC, PREC)
PREC_LAT = (lax.Precision.HIGH, lax.Precision.HIGH)


def shift_ring(value, axis, steps):
    count = lax.axis_size(axis)
    pairs = [(source, (source + steps) % count) for source in range(count)]
    return lax.ppermute(value, axis, pairs)


def all_sum(value, axis):
    count = lax.axis_size(axis)
    spread = jnp.broadcast_to(value, (count,) + value.shape)
    gathered = lax.all_to_all(spread, axis, 0, 0, tiled=True)
    total = gathered[0]
    for index in range(1, count):
        total = total + gathered[index]
    return total


def sine_basis(count):
    index = jnp.arange(count).astype(jnp.float32) + 1.0
    angle_grid = math.pi / (count + 1) * index[:, None] * index[None, :]
    table = math.sqrt(2.0 / (count + 1)) * jnp.sin(angle_grid)
    spectrum = 2.0 - 2.0 * jnp.cos(math.pi / (count + 1) * index)
    return (table, spectrum)


def transform(field, trans_x, trans_r, precs):
    inner = jnp.einsum("ij,pcjk->pcik", trans_x, field, precision=precs[0])
    return jnp.einsum("pcik,kl->pcil", inner, trans_r, precision=precs[1])


def forward(field, trans_x, trans_r, inv_real, inv_imag):
    spectral = transform(field, trans_x, trans_r, PREC_FWD)
    real_part = spectral[:, 0] * inv_real - spectral[:, 1] * inv_imag
    imag_part = spectral[:, 1] * inv_real + spectral[:, 0] * inv_imag
    return jnp.stack([real_part, imag_part], axis=1)


def precondition(field, trans_x, trans_r, inv_real, inv_imag):
    scaled = forward(field, trans_x, trans_r, inv_real, inv_imag)
    return transform(scaled, trans_x, trans_r, PREC_INV)


def lateral(field, lateral_x, lateral_r):
    padded = jnp.pad(field, ((0, 0), (0, 0), (1, 1), (1, 1)))
    stencil = (
        4.0 * field
        - padded[:, :, 2:, 1:-1]
        - padded[:, :, :-2, 1:-1]
        - padded[:, :, 1:-1, 2:]
        - padded[:, :, 1:-1, :-2]
    )
    dense = jnp.einsum("ij,pcjk->pcik", lateral_x, field, precision=PREC_LAT[0])
    dense = dense + jnp.einsum("pcik,kl->pcil", field, lateral_r, precision=PREC_LAT[1])
    return stencil + dense


def operate(field, before, after, coupling, coupling_prev, wavenumber, lateral_x, lateral_r):
    result = lateral(field, lateral_x, lateral_r) - wavenumber[:, None] * field
    result = (
        result + coupling[:, None] * (field - after) + coupling_prev[:, None] * (field - before)
    )
    return result


def on_device(source, coupling, wavenumber, lateral_x, lateral_r):
    planes = source.shape[0]
    trans_x, spec_x = sine_basis(source.shape[2])
    trans_r, spec_r = sine_basis(source.shape[3])
    denom_real = spec_x[:, None] + spec_r[None, :]
    magnitude = denom_real * denom_real + 1.0
    inv_real = denom_real / magnitude
    inv_imag = -1.0 / magnitude
    rim = shift_ring(coupling[-1:], "az", 1)
    coupling_prev = jnp.concatenate([rim, coupling[:-1]], axis=0)
    pre = lambda f: precondition(f, trans_x, trans_r, inv_real, inv_imag)
    mid = slice(1, planes - 1)
    split = planes >= 3

    def edges_of(a):
        return jnp.concatenate([a[:1], a[-1:]], axis=0)

    if split:
        residual = source
        sol_e = jnp.zeros_like(edges_of(source))
        sol_i = jnp.zeros_like(source[mid])
        c_e, c_i = edges_of(coupling), coupling[mid]
        cp_e, cp_i = edges_of(coupling_prev), coupling_prev[mid]
        w_e, w_i = edges_of(wavenumber), wavenumber[mid]
    else:
        residual = source
        solution_all = jnp.zeros_like(source)
    base = jnp.sum(source * source)

    def one_step(iteration, carry):
        residual, sol_e, sol_i, sums = carry
        scaled = forward(residual, trans_x, trans_r, inv_real, inv_imag)
        upd_e = transform(edges_of(scaled), trans_x, trans_r, PREC_INV)
        halo_before = shift_ring(upd_e[1:2], "az", 1)
        halo_after = shift_ring(upd_e[0:1], "az", -1)
        upd_i = transform(scaled[mid], trans_x, trans_r, PREC_INV)
        res_i = residual[mid]
        res_e = edges_of(residual)
        full = jnp.concatenate([upd_e[:1], upd_i, upd_e[1:]], axis=0)
        op_i = operate(
            upd_i, full[: planes - 2], full[2:], c_i, cp_i, w_i, lateral_x, lateral_r
        )
        res_i = res_i - damping * op_i
        sol_i = sol_i + damping * upd_i
        before_e = jnp.concatenate([halo_before, full[planes - 2 : planes - 1]], axis=0)
        after_e = jnp.concatenate([full[1:2], halo_after], axis=0)
        op_e = operate(upd_e, before_e, after_e, c_e, cp_e, w_e, lateral_x, lateral_r)
        res_e = res_e - damping * op_e
        sol_e = sol_e + damping * upd_e
        step_sum = jnp.sum(res_i * res_i) + jnp.sum(res_e * res_e)
        sums = lax.dynamic_update_index_in_dim(sums, step_sum, iteration, 0)
        residual = jnp.concatenate([res_e[:1], res_i, res_e[1:]], axis=0)
        return residual, sol_e, sol_i, sums

    if split:
        carry = (source, sol_e, sol_i, jnp.zeros((ITERS,), jnp.float32))
        residual, sol_e, sol_i, sums = lax.fori_loop(0, ITERS, one_step, carry)
        solution_all = jnp.concatenate([sol_e[:1], sol_i, sol_e[1:]], axis=0)
        local_sums = jnp.concatenate([base[None], sums])
    else:
        local_sums = [base]
        for iteration in range(ITERS):
            update = pre(residual)
            before = jnp.concatenate([shift_ring(update[-1:], "az", 1), update[:-1]], axis=0)
            after = jnp.concatenate([update[1:], shift_ring(update[:1], "az", -1)], axis=0)
            solution_all = solution_all + damping * update
            residual = residual - damping * operate(
                update, before, after, coupling, coupling_prev, wavenumber, lateral_x, lateral_r
            )
            local_sums.append(jnp.sum(residual * residual))
        local_sums = jnp.stack(local_sums)
    totals = all_sum(local_sums, "az")
    history = jnp.sqrt(totals[1:] / (totals[0] + epsilon))
    return (solution_all, residual, history)


def solution(mesh):
    return jax.shard_map(
        on_device,
        mesh=mesh,
        in_specs=(P("az", None, None, None), P("az", None, None), P("az", None, None), P(), P()),
        out_specs=(P("az", None, None, None), P("az", None, None, None), P()),
        check_vma=False,
    )
```

```python
import math

import jax
import jax.numpy as jnp
from jax import lax
from jax.sharding import PartitionSpec as P

ITERS = 3


damping = 0.4
epsilon = 1e-06


def from_behind(value, axis, steps):
    count = lax.axis_size(axis)
    pairs = [(source, (source + steps) % count) for source in range(count)]
    return lax.ppermute(value, axis, pairs)


def extended_2(cells, sides, width):
    for axis, dim in sides:
        count = lax.axis_size(axis)
        head = lax.slice_in_dim(cells, 0, width, axis=dim)
        tail = lax.slice_in_dim(cells, cells.shape[dim] - width, cells.shape[dim], axis=dim)
        cells = jnp.concatenate(
            [
                lax.ppermute(tail, axis, [(i, (i + 1) % count) for i in range(count)]),
                cells,
                lax.ppermute(head, axis, [((i + 1) % count, i) for i in range(count)]),
            ],
            axis=dim,
        )
    return cells


def all_sum(value, axis):
    count = lax.axis_size(axis)
    spread = jnp.broadcast_to(value, (count,) + value.shape)
    gathered = lax.all_to_all(spread, axis, 0, 0, tiled=True)
    total = gathered[0]
    for index in range(1, count):
        total = total + gathered[index]
    return total


def sine_basis(count):
    index = jnp.arange(count).astype(jnp.float32) + 1.0
    angle_grid = math.pi / (count + 1) * index[:, None] * index[None, :]
    table = math.sqrt(2.0 / (count + 1)) * jnp.sin(angle_grid)
    spectrum = 2.0 - 2.0 * jnp.cos(math.pi / (count + 1) * index)
    return (table, spectrum)


def transform(field, trans_x, trans_r):
    inner = jnp.einsum("ij,pcjk->pcik", trans_x, field, precision=lax.Precision.HIGHEST)
    return jnp.einsum("pcik,kl->pcil", inner, trans_r, precision=lax.Precision.HIGHEST)


def precondition(field, trans_x, trans_r, inv_real, inv_imag):
    spectral = transform(field, trans_x, trans_r)
    real_part = spectral[:, 0] * inv_real - spectral[:, 1] * inv_imag
    imag_part = spectral[:, 1] * inv_real + spectral[:, 0] * inv_imag
    return transform(jnp.stack([real_part, imag_part], axis=1), trans_x, trans_r)


def lateral(field, lateral_x, lateral_r):
    padded = jnp.pad(field, ((0, 0), (0, 0), (1, 1), (1, 1)))
    stencil = (
        4.0 * field
        - padded[:, :, 2:, 1:-1]
        - padded[:, :, :-2, 1:-1]
        - padded[:, :, 1:-1, 2:]
        - padded[:, :, 1:-1, :-2]
    )
    dense = jnp.einsum("ij,pcjk->pcik", lateral_x, field, precision=lax.Precision.HIGH)
    dense = dense + jnp.einsum("pcik,kl->pcil", field, lateral_r, precision=lax.Precision.HIGH)
    return stencil + dense


def operate(field, before, after, coupling, coupling_prev, wavenumber, lateral_x, lateral_r):
    result = lateral(field, lateral_x, lateral_r) - wavenumber[:, None] * field
    result = (
        result + coupling[:, None] * (field - after) + coupling_prev[:, None] * (field - before)
    )
    return result


def on_device(source, coupling, wavenumber, lateral_x, lateral_r):
    trans_x, spec_x = sine_basis(source.shape[2])
    trans_r, spec_r = sine_basis(source.shape[3])
    denom_real = spec_x[:, None] + spec_r[None, :]
    magnitude = denom_real * denom_real + 1.0
    inv_real = denom_real / magnitude
    inv_imag = -1.0 / magnitude
    rim = from_behind(coupling[-1:], "az", 1)
    coupling_prev = jnp.concatenate([rim, coupling[:-1]], axis=0)
    solution = jnp.zeros_like(source)
    residual = source
    local_base = jnp.sum(source * source)
    local_norms = []
    for iteration in range(ITERS):
        update = precondition(residual, trans_x, trans_r, inv_real, inv_imag)
        extended = extended_2(update, (("az", 0),), 1)
        before = extended[:-2]
        after = extended[2:]
        solution = solution + damping * update
        residual = residual - damping * operate(
            update, before, after, coupling, coupling_prev, wavenumber, lateral_x, lateral_r
        )
        local_sum = jnp.sum(residual * residual)
        local_norms.append(local_sum)
    totals = all_sum(jnp.stack([local_base] + local_norms), "az")
    history = jnp.sqrt(totals[1:] / (totals[0] + epsilon))
    return (solution, residual, history)


def solution(mesh):
    return jax.shard_map(
        on_device,
        mesh=mesh,
        in_specs=(P("az", None, None, None), P("az", None, None), P("az", None, None), P(), P()),
        out_specs=(P("az", None, None, None), P("az", None, None, None), P()),
        check_vma=False,
    )
```

```python
import math

import jax
import jax.numpy as jnp
from jax import lax
from jax.sharding import PartitionSpec as P

ITERS = 3


damping = 0.4
epsilon = 1e-06


def from_behind(value, axis, steps):
    count = lax.axis_size(axis)
    pairs = [(source, (source + steps) % count) for source in range(count)]
    return lax.ppermute(value, axis, pairs)


def all_sum(value, axis):
    count = lax.axis_size(axis)
    spread = jnp.broadcast_to(value, (count,) + value.shape)
    gathered = lax.all_to_all(spread, axis, 0, 0, tiled=True)
    total = gathered[0]
    for index in range(1, count):
        total = total + gathered[index]
    return total


def sine_basis(count):
    index = jnp.arange(count).astype(jnp.float32) + 1.0
    angle_grid = math.pi / (count + 1) * index[:, None] * index[None, :]
    table = math.sqrt(2.0 / (count + 1)) * jnp.sin(angle_grid)
    spectrum = 2.0 - 2.0 * jnp.cos(math.pi / (count + 1) * index)
    return (table, spectrum)


def transform(field, trans_x, trans_r):
    inner = jnp.einsum("ij,pcjk->pcik", trans_x, field, precision=lax.Precision.HIGHEST)
    return jnp.einsum("pcik,kl->pcil", inner, trans_r, precision=lax.Precision.HIGHEST)


def scaled_spectrum(field, trans_x, trans_r, inv_real, inv_imag):
    spectral = transform(field, trans_x, trans_r)
    real_part = spectral[:, 0] * inv_real - spectral[:, 1] * inv_imag
    imag_part = spectral[:, 1] * inv_real + spectral[:, 0] * inv_imag
    return jnp.stack([real_part, imag_part], axis=1)


def lateral(field, lateral_x, lateral_r):
    padded = jnp.pad(field, ((0, 0), (0, 0), (1, 1), (1, 1)))
    stencil = (
        4.0 * field
        - padded[:, :, 2:, 1:-1]
        - padded[:, :, :-2, 1:-1]
        - padded[:, :, 1:-1, 2:]
        - padded[:, :, 1:-1, :-2]
    )
    dense = jnp.einsum("ij,pcjk->pcik", lateral_x, field, precision=lax.Precision.HIGH)
    dense = dense + jnp.einsum("pcik,kl->pcil", field, lateral_r, precision=lax.Precision.HIGH)
    return stencil + dense


def operate(field, before, after, coupling, coupling_prev, wavenumber, lateral_x, lateral_r):
    result = lateral(field, lateral_x, lateral_r) - wavenumber[:, None] * field
    result = (
        result + coupling[:, None] * (field - after) + coupling_prev[:, None] * (field - before)
    )
    return result


def on_device(source, coupling, wavenumber, lateral_x, lateral_r):
    trans_x, spec_x = sine_basis(source.shape[2])
    trans_r, spec_r = sine_basis(source.shape[3])
    denom_real = spec_x[:, None] + spec_r[None, :]
    magnitude = denom_real * denom_real + 1.0
    inv_real = denom_real / magnitude
    inv_imag = -1.0 / magnitude
    rim = from_behind(coupling[-1:], "az", 1)
    coupling_prev = jnp.concatenate([rim, coupling[:-1]], axis=0)
    solution = jnp.zeros_like(source)
    residual = source
    local_base = jnp.sum(source * source)
    local_norms = []
    for iteration in range(ITERS):
        scaled = scaled_spectrum(residual, trans_x, trans_r, inv_real, inv_imag)
        halo_scaled = jnp.concatenate(
            [from_behind(scaled[-1:], "az", 1), from_behind(scaled[:1], "az", -1)], axis=0
        )
        update = transform(scaled, trans_x, trans_r)
        halo = transform(halo_scaled, trans_x, trans_r)
        before = jnp.concatenate([halo[:1], update[:-1]], axis=0)
        after = jnp.concatenate([update[1:], halo[1:]], axis=0)
        solution = solution + damping * update
        residual = residual - damping * operate(
            update, before, after, coupling, coupling_prev, wavenumber, lateral_x, lateral_r
        )
        local_sum = jnp.sum(residual * residual)
        local_norms.append(local_sum)
    totals = all_sum(jnp.stack([local_base] + local_norms), "az")
    history = jnp.sqrt(totals[1:] / (totals[0] + epsilon))
    return (solution, residual, history)


def solution(mesh):
    return jax.shard_map(
        on_device,
        mesh=mesh,
        in_specs=(P("az", None, None, None), P("az", None, None), P("az", None, None), P(), P()),
        out_specs=(P("az", None, None, None), P("az", None, None, None), P()),
        check_vma=False,
    )
```

```python
import math

import jax
import jax.numpy as jnp
from jax import lax
from jax.sharding import PartitionSpec as P

ITERS = 3


damping = 0.4
epsilon = 1e-06


def from_behind(value, axis, steps):
    count = lax.axis_size(axis)
    pairs = [(source, (source + steps) % count) for source in range(count)]
    return lax.ppermute(value, axis, pairs)


def all_sum(value, axis):
    count = lax.axis_size(axis)
    spread = jnp.broadcast_to(value, (count,) + value.shape)
    gathered = lax.all_to_all(spread, axis, 0, 0, tiled=True)
    total = gathered[0]
    for index in range(1, count):
        total = total + gathered[index]
    return total


def sine_basis(count):
    index = jnp.arange(count).astype(jnp.float32) + 1.0
    angle_grid = math.pi / (count + 1) * index[:, None] * index[None, :]
    table = math.sqrt(2.0 / (count + 1)) * jnp.sin(angle_grid)
    spectrum = 2.0 - 2.0 * jnp.cos(math.pi / (count + 1) * index)
    return (table, spectrum)


def transform(field, trans_x, trans_r):
    inner = jnp.einsum("ij,pcjk->pcik", trans_x, field, precision=lax.Precision.HIGHEST)
    return jnp.einsum("pcik,kl->pcil", inner, trans_r, precision=lax.Precision.HIGHEST)


def scaled_spectrum(field, trans_x, trans_r, inv_real, inv_imag):
    spectral = transform(field, trans_x, trans_r)
    real_part = spectral[:, 0] * inv_real - spectral[:, 1] * inv_imag
    imag_part = spectral[:, 1] * inv_real + spectral[:, 0] * inv_imag
    return jnp.stack([real_part, imag_part], axis=1)


def lateral(field, lateral_x, lateral_r):
    padded = jnp.pad(field, ((0, 0), (0, 0), (1, 1), (1, 1)))
    stencil = (
        4.0 * field
        - padded[:, :, 2:, 1:-1]
        - padded[:, :, :-2, 1:-1]
        - padded[:, :, 1:-1, 2:]
        - padded[:, :, 1:-1, :-2]
    )
    dense = jnp.einsum("ij,pcjk->pcik", lateral_x, field, precision=lax.Precision.HIGH)
    dense = dense + jnp.einsum("pcik,kl->pcil", field, lateral_r, precision=lax.Precision.HIGH)
    return stencil + dense


def operate(field, before, after, coupling, coupling_prev, wavenumber, lateral_x, lateral_r):
    result = lateral(field, lateral_x, lateral_r) - wavenumber[:, None] * field
    result = (
        result + coupling[:, None] * (field - after) + coupling_prev[:, None] * (field - before)
    )
    return result


def on_device(source, coupling, wavenumber, lateral_x, lateral_r):
    trans_x, spec_x = sine_basis(source.shape[2])
    trans_r, spec_r = sine_basis(source.shape[3])
    denom_real = spec_x[:, None] + spec_r[None, :]
    magnitude = denom_real * denom_real + 1.0
    inv_real = denom_real / magnitude
    inv_imag = -1.0 / magnitude
    trans_x, trans_r, inv_real, inv_imag = lax.optimization_barrier(
        (trans_x, trans_r, inv_real, inv_imag)
    )
    solution = jnp.zeros_like(source)
    residual = source
    local_base = jnp.sum(source * source)
    local_norms = []
    for iteration in range(ITERS):
        scaled = scaled_spectrum(residual, trans_x, trans_r, inv_real, inv_imag)
        if iteration == 0:
            sent = jnp.concatenate([scaled[-1:], coupling[-1:, None]], axis=1)
            got = from_behind(sent, "az", 1)
            from_before = got[:, :2]
            coupling_prev = jnp.concatenate([got[:, 2], coupling[:-1]], axis=0)
        else:
            from_before = from_behind(scaled[-1:], "az", 1)
        halo_scaled = jnp.concatenate([from_before, from_behind(scaled[:1], "az", -1)], axis=0)
        update = transform(scaled, trans_x, trans_r)
        halo = transform(halo_scaled, trans_x, trans_r)
        before = jnp.concatenate([halo[:1], update[:-1]], axis=0)
        after = jnp.concatenate([update[1:], halo[1:]], axis=0)
        solution = solution + damping * update
        residual = residual - damping * operate(
            update, before, after, coupling, coupling_prev, wavenumber, lateral_x, lateral_r
        )
        local_sum = jnp.sum(residual * residual)
        local_norms.append(local_sum)
    totals = all_sum(jnp.stack([local_base] + local_norms), "az")
    history = jnp.sqrt(totals[1:] / (totals[0] + epsilon))
    return (solution, residual, history)


def solution(mesh):
    return jax.shard_map(
        on_device,
        mesh=mesh,
        in_specs=(P("az", None, None, None), P("az", None, None), P("az", None, None), P(), P()),
        out_specs=(P("az", None, None, None), P("az", None, None, None), P()),
        check_vma=False,
    )
```

```python
import math

import jax
import jax.numpy as jnp
from jax import lax
from jax.sharding import PartitionSpec as P

ITERS = 3


damping = 0.4
epsilon = 1e-06


def from_behind(value, axis, steps):
    count = lax.axis_size(axis)
    pairs = [(source, (source + steps) % count) for source in range(count)]
    return lax.ppermute(value, axis, pairs)


def all_sum(value, axis):
    count = lax.axis_size(axis)
    spread = jnp.broadcast_to(value, (count,) + value.shape)
    gathered = lax.all_to_all(spread, axis, 0, 0, tiled=True)
    total = gathered[0]
    for index in range(1, count):
        total = total + gathered[index]
    return total


def sine_basis(count):
    index = jnp.arange(count).astype(jnp.float32) + 1.0
    angle_grid = math.pi / (count + 1) * index[:, None] * index[None, :]
    table = math.sqrt(2.0 / (count + 1)) * jnp.sin(angle_grid)
    spectrum = 2.0 - 2.0 * jnp.cos(math.pi / (count + 1) * index)
    return (table, spectrum)


def transform(field, trans_x, trans_r):
    inner = jnp.einsum("ij,pcjk->pcik", trans_x, field, precision=lax.Precision.HIGHEST)
    return jnp.einsum("pcik,kl->pcil", inner, trans_r, precision=lax.Precision.HIGHEST)


def scaled_spectrum(field, trans_x, trans_r, inv_real, inv_imag):
    spectral = transform(field, trans_x, trans_r)
    real_part = spectral[:, 0] * inv_real - spectral[:, 1] * inv_imag
    imag_part = spectral[:, 1] * inv_real + spectral[:, 0] * inv_imag
    return jnp.stack([real_part, imag_part], axis=1)


def lateral(field, lateral_x, lateral_r):
    padded = jnp.pad(field, ((0, 0), (0, 0), (1, 1), (1, 1)))
    stencil = (
        4.0 * field
        - padded[:, :, 2:, 1:-1]
        - padded[:, :, :-2, 1:-1]
        - padded[:, :, 1:-1, 2:]
        - padded[:, :, 1:-1, :-2]
    )
    dense = jnp.einsum("ij,pcjk->pcik", lateral_x, field, precision=lax.Precision.HIGH)
    dense = dense + jnp.einsum("pcik,kl->pcil", field, lateral_r, precision=lax.Precision.HIGH)
    return stencil + dense


def operate(field, before, after, coupling, coupling_prev, wavenumber, lateral_x, lateral_r):
    result = lateral(field, lateral_x, lateral_r) - wavenumber[:, None] * field
    result = (
        result + coupling[:, None] * (field - after) + coupling_prev[:, None] * (field - before)
    )
    return result


def on_device(source, coupling, wavenumber, lateral_x, lateral_r):
    trans_x, spec_x = sine_basis(source.shape[2])
    trans_r, spec_r = sine_basis(source.shape[3])
    denom_real = spec_x[:, None] + spec_r[None, :]
    magnitude = denom_real * denom_real + 1.0
    inv_real = denom_real / magnitude
    inv_imag = -1.0 / magnitude
    trans_x, trans_r, inv_real, inv_imag = lax.optimization_barrier(
        (trans_x, trans_r, inv_real, inv_imag)
    )
    solution = jnp.zeros_like(source)
    residual = source
    local_base = jnp.sum(source * source)
    local_norms = []
    for iteration in range(ITERS):
        scaled = scaled_spectrum(residual, trans_x, trans_r, inv_real, inv_imag)
        if iteration == 0:
            sent = jnp.concatenate([scaled[-1:], coupling[-1:, None]], axis=1)
            got = from_behind(sent, "az", 1)
            from_before = got[:, :2]
            coupling_prev = lax.optimization_barrier(
                jnp.concatenate([got[:, 2], coupling[:-1]], axis=0)
            )
        else:
            from_before = from_behind(scaled[-1:], "az", 1)
        halo_scaled = jnp.concatenate([from_before, from_behind(scaled[:1], "az", -1)], axis=0)
        update = transform(scaled, trans_x, trans_r)
        halo = transform(halo_scaled, trans_x, trans_r)
        extended = lax.optimization_barrier(
            jnp.concatenate([halo[:1], update, halo[1:]], axis=0)
        )
        before = extended[:-2]
        after = extended[2:]
        solution = solution + damping * update
        residual = residual - damping * operate(
            update, before, after, coupling, coupling_prev, wavenumber, lateral_x, lateral_r
        )
        local_sum = jnp.sum(residual * residual)
        local_norms.append(local_sum)
    totals = all_sum(jnp.stack([local_base] + local_norms), "az")
    history = jnp.sqrt(totals[1:] / (totals[0] + epsilon))
    return (solution, residual, history)


def solution(mesh):
    return jax.shard_map(
        on_device,
        mesh=mesh,
        in_specs=(P("az", None, None, None), P("az", None, None), P("az", None, None), P(), P()),
        out_specs=(P("az", None, None, None), P("az", None, None, None), P()),
        check_vma=False,
    )
```

```python
import math

import jax
import jax.numpy as jnp
from jax import lax
from jax.sharding import PartitionSpec as P

ITERS = 3


damping = 0.4
epsilon = 1e-06


def from_behind(value, axis, steps):
    count = lax.axis_size(axis)
    pairs = [(source, (source + steps) % count) for source in range(count)]
    return lax.ppermute(value, axis, pairs)


def all_sum(value, axis):
    count = lax.axis_size(axis)
    spread = jnp.broadcast_to(value, (count,) + value.shape)
    gathered = lax.all_to_all(spread, axis, 0, 0, tiled=True)
    total = gathered[0]
    for index in range(1, count):
        total = total + gathered[index]
    return total


def sine_basis(count):
    index = jnp.arange(count).astype(jnp.float32) + 1.0
    angle_grid = math.pi / (count + 1) * index[:, None] * index[None, :]
    table = math.sqrt(2.0 / (count + 1)) * jnp.sin(angle_grid)
    spectrum = 2.0 - 2.0 * jnp.cos(math.pi / (count + 1) * index)
    return (table, spectrum)


def transform(field, trans_x, trans_r):
    inner = jnp.einsum("ij,pcjk->pcik", trans_x, field, precision=lax.Precision.HIGHEST)
    return jnp.einsum("pcik,kl->pcil", inner, trans_r, precision=lax.Precision.HIGHEST)


def scaled_spectrum(field, trans_x, trans_r, inv_real, inv_imag):
    spectral = transform(field, trans_x, trans_r)
    real_part = spectral[:, 0] * inv_real - spectral[:, 1] * inv_imag
    imag_part = spectral[:, 1] * inv_real + spectral[:, 0] * inv_imag
    return jnp.stack([real_part, imag_part], axis=1)


def lateral(field, lateral_x, lateral_r):
    padded = jnp.pad(field, ((0, 0), (0, 0), (1, 1), (1, 1)))
    stencil = (
        4.0 * field
        - padded[:, :, 2:, 1:-1]
        - padded[:, :, :-2, 1:-1]
        - padded[:, :, 1:-1, 2:]
        - padded[:, :, 1:-1, :-2]
    )
    dense = jnp.einsum("ij,pcjk->pcik", lateral_x, field, precision=lax.Precision.HIGH)
    dense = dense + jnp.einsum("pcik,kl->pcil", field, lateral_r, precision=lax.Precision.HIGH)
    return stencil + dense


def operate(field, before, after, coupling, coupling_prev, wavenumber, lateral_x, lateral_r):
    result = lateral(field, lateral_x, lateral_r) - wavenumber[:, None] * field
    result = (
        result + coupling[:, None] * (field - after) + coupling_prev[:, None] * (field - before)
    )
    return result


def on_device(source, coupling, wavenumber, lateral_x, lateral_r):
    trans_x, spec_x = sine_basis(source.shape[2])
    trans_r, spec_r = sine_basis(source.shape[3])
    denom_real = spec_x[:, None] + spec_r[None, :]
    magnitude = denom_real * denom_real + 1.0
    inv_real = denom_real / magnitude
    inv_imag = -1.0 / magnitude
    trans_x, trans_r, inv_real, inv_imag = lax.optimization_barrier(
        (trans_x, trans_r, inv_real, inv_imag)
    )
    solution = jnp.zeros_like(source)
    residual = source
    local_base = jnp.sum(source * source)
    local_norms = []
    early = None
    for iteration in range(ITERS):
        if iteration == ITERS - 1:
            early, residual = lax.optimization_barrier(
                (jnp.stack([local_base] + local_norms), residual)
            )
        scaled = scaled_spectrum(residual, trans_x, trans_r, inv_real, inv_imag)
        if iteration == 0:
            sent = jnp.concatenate([scaled[-1:], coupling[-1:, None]], axis=1)
            got = from_behind(sent, "az", 1)
            from_before = got[:, :2]
            coupling_prev = lax.optimization_barrier(
                jnp.concatenate([got[:, 2], coupling[:-1]], axis=0)
            )
        else:
            from_before = from_behind(scaled[-1:], "az", 1)
        halo_scaled = jnp.concatenate([from_before, from_behind(scaled[:1], "az", -1)], axis=0)
        update = transform(scaled, trans_x, trans_r)
        halo = transform(halo_scaled, trans_x, trans_r)
        extended = lax.optimization_barrier(
            jnp.concatenate([halo[:1], update, halo[1:]], axis=0)
        )
        before = extended[:-2]
        after = extended[2:]
        solution = solution + damping * update
        residual = residual - damping * operate(
            update, before, after, coupling, coupling_prev, wavenumber, lateral_x, lateral_r
        )
        local_sum = jnp.sum(residual * residual)
        local_norms.append(local_sum)
    totals = all_sum(jnp.concatenate([early, local_norms[-1][None]]), "az")
    history = jnp.sqrt(totals[1:] / (totals[0] + epsilon))
    return (solution, residual, history)


def solution(mesh):
    return jax.shard_map(
        on_device,
        mesh=mesh,
        in_specs=(P("az", None, None, None), P("az", None, None), P("az", None, None), P(), P()),
        out_specs=(P("az", None, None, None), P("az", None, None, None), P()),
        check_vma=False,
    )
```

```python
import math

import jax
import jax.numpy as jnp
from jax import lax
from jax.sharding import PartitionSpec as P

ITERS = 3


damping = 0.4
epsilon = 1e-06


def from_behind(value, axis, steps):
    count = lax.axis_size(axis)
    pairs = [(source, (source + steps) % count) for source in range(count)]
    return lax.ppermute(value, axis, pairs)


def all_sum(value, axis):
    count = lax.axis_size(axis)
    spread = jnp.broadcast_to(value, (count,) + value.shape)
    gathered = lax.all_to_all(spread, axis, 0, 0, tiled=True)
    total = gathered[0]
    for index in range(1, count):
        total = total + gathered[index]
    return total


def sine_basis(count):
    index = jnp.arange(count).astype(jnp.float32) + 1.0
    angle_grid = math.pi / (count + 1) * index[:, None] * index[None, :]
    table = math.sqrt(2.0 / (count + 1)) * jnp.sin(angle_grid)
    spectrum = 2.0 - 2.0 * jnp.cos(math.pi / (count + 1) * index)
    return (table, spectrum)


def transform(field, trans_x, trans_r):
    inner = jnp.einsum("ij,pcjk->pcik", trans_x, field, precision=lax.Precision.HIGHEST)
    return jnp.einsum("pcik,kl->pcil", inner, trans_r, precision=lax.Precision.HIGHEST)


def scaled_spectrum(field, trans_x, trans_r, inv_real, inv_imag):
    spectral = transform(field, trans_x, trans_r)
    real_part = spectral[:, 0] * inv_real - spectral[:, 1] * inv_imag
    imag_part = spectral[:, 1] * inv_real + spectral[:, 0] * inv_imag
    return jnp.stack([real_part, imag_part], axis=1)


def lateral(field, lateral_x, lateral_r):
    padded = jnp.pad(field, ((0, 0), (0, 0), (1, 1), (1, 1)))
    stencil = (
        4.0 * field
        - padded[:, :, 2:, 1:-1]
        - padded[:, :, :-2, 1:-1]
        - padded[:, :, 1:-1, 2:]
        - padded[:, :, 1:-1, :-2]
    )
    dense = jnp.einsum("ij,pcjk->pcik", lateral_x, field, precision=lax.Precision.HIGH)
    dense = dense + jnp.einsum("pcik,kl->pcil", field, lateral_r, precision=lax.Precision.HIGH)
    return stencil + dense


def operate(field, before, after, coupling, coupling_prev, wavenumber, lateral_x, lateral_r):
    result = lateral(field, lateral_x, lateral_r) - wavenumber[:, None] * field
    result = (
        result + coupling[:, None] * (field - after) + coupling_prev[:, None] * (field - before)
    )
    return result


def on_device(source, coupling, wavenumber, lateral_x, lateral_r):
    trans_x, spec_x = sine_basis(source.shape[2])
    trans_r, spec_r = sine_basis(source.shape[3])
    denom_real = spec_x[:, None] + spec_r[None, :]
    magnitude = denom_real * denom_real + 1.0
    inv_real = denom_real / magnitude
    inv_imag = -1.0 / magnitude
    trans_x, trans_r, inv_real, inv_imag = lax.optimization_barrier(
        (trans_x, trans_r, inv_real, inv_imag)
    )
    solution = jnp.zeros_like(source)
    residual = source
    local_base = jnp.sum(source * source)
    local_norms = []
    early = None
    for iteration in range(ITERS):
        if iteration == ITERS - 1:
            early, residual = lax.optimization_barrier(
                (jnp.stack([local_base] + local_norms), residual)
            )
        scaled = scaled_spectrum(residual, trans_x, trans_r, inv_real, inv_imag)
        if iteration == 0:
            sent = jnp.concatenate([scaled[-1:], coupling[-1:, None]], axis=1)
            got = from_behind(sent, "az", 1)
            from_before = got[:, :2]
            coupling_prev = lax.optimization_barrier(
                jnp.concatenate([got[:, 2], coupling[:-1]], axis=0)
            )
        else:
            from_before = from_behind(scaled[-1:], "az", 1)
        halo_scaled = jnp.concatenate([from_before, from_behind(scaled[:1], "az", -1)], axis=0)
        update = transform(scaled, trans_x, trans_r)
        blank = jnp.zeros_like(update[:1])
        before = jnp.concatenate([blank, update[:-1]], axis=0)
        after = jnp.concatenate([update[1:], blank], axis=0)
        solution = solution + damping * update
        residual = residual - damping * operate(
            update, before, after, coupling, coupling_prev, wavenumber, lateral_x, lateral_r
        )
        halo = transform(halo_scaled, trans_x, trans_r)
        residual = residual.at[:1].add(damping * (coupling_prev[:1, None] * halo[:1]))
        residual = residual.at[-1:].add(damping * (coupling[-1:, None] * halo[1:]))
        local_sum = jnp.sum(residual * residual)
        local_norms.append(local_sum)
    totals = all_sum(jnp.concatenate([early, local_norms[-1][None]]), "az")
    history = jnp.sqrt(totals[1:] / (totals[0] + epsilon))
    return (solution, residual, history)


def solution(mesh):
    return jax.shard_map(
        on_device,
        mesh=mesh,
        in_specs=(P("az", None, None, None), P("az", None, None), P("az", None, None), P(), P()),
        out_specs=(P("az", None, None, None), P("az", None, None, None), P()),
        check_vma=False,
    )
```

```python
import math

import jax
import jax.numpy as jnp
from jax import lax
from jax.sharding import PartitionSpec as P

ITERS = 3


damping = 0.4
epsilon = 1e-06


def from_behind(value, axis, steps):
    count = lax.axis_size(axis)
    pairs = [(source, (source + steps) % count) for source in range(count)]
    return lax.ppermute(value, axis, pairs)


def all_sum(value, axis):
    count = lax.axis_size(axis)
    spread = jnp.broadcast_to(value, (count,) + value.shape)
    gathered = lax.all_to_all(spread, axis, 0, 0, tiled=True)
    total = gathered[0]
    for index in range(1, count):
        total = total + gathered[index]
    return total


def sine_basis(count):
    index = jnp.arange(count).astype(jnp.float32) + 1.0
    angle_grid = math.pi / (count + 1) * index[:, None] * index[None, :]
    table = math.sqrt(2.0 / (count + 1)) * jnp.sin(angle_grid)
    spectrum = 2.0 - 2.0 * jnp.cos(math.pi / (count + 1) * index)
    return (table, spectrum)


def transform(field, trans_x, trans_r, precision=lax.Precision.HIGHEST):
    inner = jnp.einsum("ij,pcjk->pcik", trans_x, field, precision=precision)
    return jnp.einsum("pcik,kl->pcil", inner, trans_r, precision=precision)


def scaled_spectrum(field, trans_x, trans_r, inv_real, inv_imag):
    spectral = transform(field, trans_x, trans_r)
    real_part = spectral[:, 0] * inv_real - spectral[:, 1] * inv_imag
    imag_part = spectral[:, 1] * inv_real + spectral[:, 0] * inv_imag
    return jnp.stack([real_part, imag_part], axis=1)


def lateral(field, lateral_x, lateral_r):
    padded = jnp.pad(field, ((0, 0), (0, 0), (1, 1), (1, 1)))
    stencil = (
        4.0 * field
        - padded[:, :, 2:, 1:-1]
        - padded[:, :, :-2, 1:-1]
        - padded[:, :, 1:-1, 2:]
        - padded[:, :, 1:-1, :-2]
    )
    dense = jnp.einsum("ij,pcjk->pcik", lateral_x, field, precision=lax.Precision.HIGH)
    dense = dense + jnp.einsum("pcik,kl->pcil", field, lateral_r, precision=lax.Precision.HIGH)
    return stencil + dense


def operate(field, before, after, coupling, coupling_prev, wavenumber, lateral_x, lateral_r):
    result = lateral(field, lateral_x, lateral_r) - wavenumber[:, None] * field
    result = (
        result + coupling[:, None] * (field - after) + coupling_prev[:, None] * (field - before)
    )
    return result


def on_device(source, coupling, wavenumber, lateral_x, lateral_r):
    trans_x, spec_x = sine_basis(source.shape[2])
    trans_r, spec_r = sine_basis(source.shape[3])
    denom_real = spec_x[:, None] + spec_r[None, :]
    magnitude = denom_real * denom_real + 1.0
    inv_real = denom_real / magnitude
    inv_imag = -1.0 / magnitude
    trans_x, trans_r, inv_real, inv_imag = lax.optimization_barrier(
        (trans_x, trans_r, inv_real, inv_imag)
    )
    solution = jnp.zeros_like(source)
    residual = source
    local_base = jnp.sum(source * source)
    local_norms = []
    for iteration in range(ITERS):
        scaled = scaled_spectrum(residual, trans_x, trans_r, inv_real, inv_imag)
        if iteration == 0:
            sent = jnp.concatenate([scaled[-1:], coupling[-1:, None]], axis=1)
            got = from_behind(sent, "az", 1)
            from_before = got[:, :2]
            coupling_prev = lax.optimization_barrier(
                jnp.concatenate([got[:, 2], coupling[:-1]], axis=0)
            )
        else:
            from_before = from_behind(scaled[-1:], "az", 1)
        halo_scaled = jnp.concatenate([from_before, from_behind(scaled[:1], "az", -1)], axis=0)
        update = transform(scaled, trans_x, trans_r)
        halo = transform(halo_scaled, trans_x, trans_r, lax.Precision.HIGH)
        extended = lax.optimization_barrier(
            jnp.concatenate([halo[:1], update, halo[1:]], axis=0)
        )
        before = extended[:-2]
        after = extended[2:]
        solution = solution + damping * update
        residual = residual - damping * operate(
            update, before, after, coupling, coupling_prev, wavenumber, lateral_x, lateral_r
        )
        local_sum = jnp.sum(residual * residual)
        local_norms.append(local_sum)
    totals = all_sum(jnp.stack([local_base] + local_norms), "az")
    history = jnp.sqrt(totals[1:] / (totals[0] + epsilon))
    return (solution, residual, history)


def solution(mesh):
    return jax.shard_map(
        on_device,
        mesh=mesh,
        in_specs=(P("az", None, None, None), P("az", None, None), P("az", None, None), P(), P()),
        out_specs=(P("az", None, None, None), P("az", None, None, None), P()),
        check_vma=False,
    )
```

```python
import math

import jax
import jax.numpy as jnp
from jax import lax
from jax.sharding import PartitionSpec as P

ITERS = 3


damping = 0.4
epsilon = 1e-06


def from_behind(value, axis, steps):
    count = lax.axis_size(axis)
    pairs = [(source, (source + steps) % count) for source in range(count)]
    return lax.ppermute(value, axis, pairs)


def all_sum(value, axis):
    count = lax.axis_size(axis)
    spread = jnp.broadcast_to(value, (count,) + value.shape)
    gathered = lax.all_to_all(spread, axis, 0, 0, tiled=True)
    total = gathered[0]
    for index in range(1, count):
        total = total + gathered[index]
    return total


def sine_basis(count):
    index = jnp.arange(count).astype(jnp.float32) + 1.0
    angle_grid = math.pi / (count + 1) * index[:, None] * index[None, :]
    table = math.sqrt(2.0 / (count + 1)) * jnp.sin(angle_grid)
    spectrum = 2.0 - 2.0 * jnp.cos(math.pi / (count + 1) * index)
    return (table, spectrum)


def transform(field, trans_x, trans_r, precision=lax.Precision.HIGHEST):
    inner = jnp.einsum("ij,pcjk->pcik", trans_x, field, precision=precision)
    return jnp.einsum("pcik,kl->pcil", inner, trans_r, precision=precision)


def scaled_spectrum(field, trans_x, trans_r, inv_real, inv_imag):
    spectral = transform(field, trans_x, trans_r)
    real_part = spectral[:, 0] * inv_real - spectral[:, 1] * inv_imag
    imag_part = spectral[:, 1] * inv_real + spectral[:, 0] * inv_imag
    return jnp.stack([real_part, imag_part], axis=1)


def lateral(field, lateral_x, lateral_r):
    padded = jnp.pad(field, ((0, 0), (0, 0), (1, 1), (1, 1)))
    stencil = (
        4.0 * field
        - padded[:, :, 2:, 1:-1]
        - padded[:, :, :-2, 1:-1]
        - padded[:, :, 1:-1, 2:]
        - padded[:, :, 1:-1, :-2]
    )
    dense = jnp.einsum("ij,pcjk->pcik", lateral_x, field, precision=lax.Precision.HIGH)
    dense = dense + jnp.einsum("pcik,kl->pcil", field, lateral_r, precision=lax.Precision.HIGH)
    return stencil + dense


def operate(field, before, after, coupling, coupling_prev, wavenumber, lateral_x, lateral_r):
    result = lateral(field, lateral_x, lateral_r) - wavenumber[:, None] * field
    result = (
        result + coupling[:, None] * (field - after) + coupling_prev[:, None] * (field - before)
    )
    return result


def on_device(source, coupling, wavenumber, lateral_x, lateral_r):
    trans_x, spec_x = sine_basis(source.shape[2])
    trans_r, spec_r = sine_basis(source.shape[3])
    denom_real = spec_x[:, None] + spec_r[None, :]
    magnitude = denom_real * denom_real + 1.0
    inv_real = denom_real / magnitude
    inv_imag = -1.0 / magnitude
    trans_x, trans_r, inv_real, inv_imag = lax.optimization_barrier(
        (trans_x, trans_r, inv_real, inv_imag)
    )
    solution = jnp.zeros_like(source)
    residual = source
    local_base = jnp.sum(source * source)
    local_norms = []
    for iteration in range(ITERS):
        scaled = scaled_spectrum(residual, trans_x, trans_r, inv_real, inv_imag)
        inner = jnp.einsum("ij,pcjk->pcik", trans_x, scaled, precision=lax.Precision.HIGHEST)
        if iteration == 0:
            sent = jnp.concatenate([inner[-1:], coupling[-1:, None]], axis=1)
            got = from_behind(sent, "az", 1)
            from_before = got[:, :2]
            coupling_prev = lax.optimization_barrier(
                jnp.concatenate([got[:, 2], coupling[:-1]], axis=0)
            )
        else:
            from_before = from_behind(inner[-1:], "az", 1)
        halo_inner = jnp.concatenate([from_before, from_behind(inner[:1], "az", -1)], axis=0)
        update = jnp.einsum("pcik,kl->pcil", inner, trans_r, precision=lax.Precision.HIGHEST)
        halo = jnp.einsum("pcik,kl->pcil", halo_inner, trans_r, precision=lax.Precision.HIGH)
        extended = lax.optimization_barrier(
            jnp.concatenate([halo[:1], update, halo[1:]], axis=0)
        )
        before = extended[:-2]
        after = extended[2:]
        solution = solution + damping * update
        residual = residual - damping * operate(
            update, before, after, coupling, coupling_prev, wavenumber, lateral_x, lateral_r
        )
        local_sum = jnp.sum(residual * residual)
        local_norms.append(local_sum)
    totals = all_sum(jnp.stack([local_base] + local_norms), "az")
    history = jnp.sqrt(totals[1:] / (totals[0] + epsilon))
    return (solution, residual, history)


def solution(mesh):
    return jax.shard_map(
        on_device,
        mesh=mesh,
        in_specs=(P("az", None, None, None), P("az", None, None), P("az", None, None), P(), P()),
        out_specs=(P("az", None, None, None), P("az", None, None, None), P()),
        check_vma=False,
    )
```

```python
import math

import jax
import jax.numpy as jnp
from jax import lax
from jax.sharding import PartitionSpec as P

ITERS = 3


damping = 0.4
epsilon = 1e-06


def from_behind(value, axis, steps):
    count = lax.axis_size(axis)
    pairs = [(source, (source + steps) % count) for source in range(count)]
    return lax.ppermute(value, axis, pairs)


def all_sum(value, axis):
    count = lax.axis_size(axis)
    spread = jnp.broadcast_to(value, (count,) + value.shape)
    gathered = lax.all_to_all(spread, axis, 0, 0, tiled=True)
    total = gathered[0]
    for index in range(1, count):
        total = total + gathered[index]
    return total


def sine_basis(count):
    index = jnp.arange(count).astype(jnp.float32) + 1.0
    angle_grid = math.pi / (count + 1) * index[:, None] * index[None, :]
    table = math.sqrt(2.0 / (count + 1)) * jnp.sin(angle_grid)
    spectrum = 2.0 - 2.0 * jnp.cos(math.pi / (count + 1) * index)
    return (table, spectrum)


def transform(field, trans_x, trans_r, precision=lax.Precision.HIGHEST):
    inner = jnp.einsum("ij,pcjk->pcik", trans_x, field, precision=precision)
    return jnp.einsum("pcik,kl->pcil", inner, trans_r, precision=precision)


def scaled_spectrum(field, trans_x, trans_r, inv_real, inv_imag):
    spectral = transform(field, trans_x, trans_r)
    real_part = spectral[:, 0] * inv_real - spectral[:, 1] * inv_imag
    imag_part = spectral[:, 1] * inv_real + spectral[:, 0] * inv_imag
    return jnp.stack([real_part, imag_part], axis=1)


def lateral(field, lateral_x, lateral_r):
    padded = jnp.pad(field, ((0, 0), (0, 0), (1, 1), (1, 1)))
    stencil = (
        4.0 * field
        - padded[:, :, 2:, 1:-1]
        - padded[:, :, :-2, 1:-1]
        - padded[:, :, 1:-1, 2:]
        - padded[:, :, 1:-1, :-2]
    )
    dense = jnp.einsum("ij,pcjk->pcik", lateral_x, field, precision=lax.Precision.HIGH)
    dense = dense + jnp.einsum("pcik,kl->pcil", field, lateral_r, precision=lax.Precision.HIGH)
    return stencil + dense


def operate(field, before, after, coupling, coupling_prev, wavenumber, lateral_x, lateral_r):
    local = lax.optimization_barrier(lateral(field, lateral_x, lateral_r))
    result = local - wavenumber[:, None] * field
    result = (
        result + coupling[:, None] * (field - after) + coupling_prev[:, None] * (field - before)
    )
    return result


def on_device(source, coupling, wavenumber, lateral_x, lateral_r):
    trans_x, spec_x = sine_basis(source.shape[2])
    trans_r, spec_r = sine_basis(source.shape[3])
    denom_real = spec_x[:, None] + spec_r[None, :]
    magnitude = denom_real * denom_real + 1.0
    inv_real = denom_real / magnitude
    inv_imag = -1.0 / magnitude
    trans_x, trans_r, inv_real, inv_imag = lax.optimization_barrier(
        (trans_x, trans_r, inv_real, inv_imag)
    )
    solution = jnp.zeros_like(source)
    residual = source
    local_base = jnp.sum(source * source)
    local_norms = []
    for iteration in range(ITERS):
        scaled = scaled_spectrum(residual, trans_x, trans_r, inv_real, inv_imag)
        if iteration == 0:
            sent = jnp.concatenate([scaled[-1:], coupling[-1:, None]], axis=1)
            got = from_behind(sent, "az", 1)
            from_before = got[:, :2]
            coupling_prev = lax.optimization_barrier(
                jnp.concatenate([got[:, 2], coupling[:-1]], axis=0)
            )
        else:
            from_before = from_behind(scaled[-1:], "az", 1)
        halo_scaled = jnp.concatenate([from_before, from_behind(scaled[:1], "az", -1)], axis=0)
        update = transform(scaled, trans_x, trans_r)
        halo = transform(halo_scaled, trans_x, trans_r, lax.Precision.HIGH)
        extended = lax.optimization_barrier(
            jnp.concatenate([halo[:1], update, halo[1:]], axis=0)
        )
        before = extended[:-2]
        after = extended[2:]
        solution = solution + damping * update
        residual = residual - damping * operate(
            update, before, after, coupling, coupling_prev, wavenumber, lateral_x, lateral_r
        )
        local_sum = jnp.sum(residual * residual)
        local_norms.append(local_sum)
    totals = all_sum(jnp.stack([local_base] + local_norms), "az")
    history = jnp.sqrt(totals[1:] / (totals[0] + epsilon))
    return (solution, residual, history)


def solution(mesh):
    return jax.shard_map(
        on_device,
        mesh=mesh,
        in_specs=(P("az", None, None, None), P("az", None, None), P("az", None, None), P(), P()),
        out_specs=(P("az", None, None, None), P("az", None, None, None), P()),
        check_vma=False,
    )
```

```python
import math

import jax
import jax.numpy as jnp
from jax import lax
from jax.sharding import PartitionSpec as P

ITERS = 3


damping = 0.4
epsilon = 1e-06


def from_behind(value, axis, steps):
    count = lax.axis_size(axis)
    pairs = [(source, (source + steps) % count) for source in range(count)]
    return lax.ppermute(value, axis, pairs)


def all_sum(value, axis):
    count = lax.axis_size(axis)
    spread = jnp.broadcast_to(value, (count,) + value.shape)
    gathered = lax.all_to_all(spread, axis, 0, 0, tiled=True)
    total = gathered[0]
    for index in range(1, count):
        total = total + gathered[index]
    return total


def sine_basis(count):
    index = jnp.arange(count).astype(jnp.float32) + 1.0
    angle_grid = math.pi / (count + 1) * index[:, None] * index[None, :]
    table = math.sqrt(2.0 / (count + 1)) * jnp.sin(angle_grid)
    spectrum = 2.0 - 2.0 * jnp.cos(math.pi / (count + 1) * index)
    return (table, spectrum)


def transform(field, trans_x, trans_r, precision=lax.Precision.HIGHEST):
    inner = jnp.einsum("ij,pcjk->pcik", trans_x, field, precision=precision)
    return jnp.einsum("pcik,kl->pcil", inner, trans_r, precision=precision)


def scaled_spectrum(field, trans_x, trans_r, inv_real, inv_imag):
    spectral = transform(field, trans_x, trans_r)
    real_part = spectral[:, 0] * inv_real - spectral[:, 1] * inv_imag
    imag_part = spectral[:, 1] * inv_real + spectral[:, 0] * inv_imag
    return jnp.stack([real_part, imag_part], axis=1)


def lateral(field, lateral_x, lateral_r):
    padded = jnp.pad(field, ((0, 0), (0, 0), (1, 1), (1, 1)))
    stencil = (
        4.0 * field
        - padded[:, :, 2:, 1:-1]
        - padded[:, :, :-2, 1:-1]
        - padded[:, :, 1:-1, 2:]
        - padded[:, :, 1:-1, :-2]
    )
    dense = jnp.einsum("ij,pcjk->pcik", lateral_x, field, precision=lax.Precision.HIGH)
    dense = dense + jnp.einsum("pcik,kl->pcil", field, lateral_r, precision=lax.Precision.HIGH)
    return stencil + dense


def operate(field, before, after, coupling, coupling_prev, wavenumber, lateral_x, lateral_r):
    result = lateral(field, lateral_x, lateral_r) - wavenumber[:, None] * field
    result = (
        result + coupling[:, None] * (field - after) + coupling_prev[:, None] * (field - before)
    )
    return result


def on_device(source, coupling, wavenumber, lateral_x, lateral_r):
    trans_x, spec_x = sine_basis(source.shape[2])
    trans_r, spec_r = sine_basis(source.shape[3])
    denom_real = spec_x[:, None] + spec_r[None, :]
    magnitude = denom_real * denom_real + 1.0
    inv_real = denom_real / magnitude
    inv_imag = -1.0 / magnitude
    trans_x, trans_r, inv_real, inv_imag = lax.optimization_barrier(
        (trans_x, trans_r, inv_real, inv_imag)
    )
    solution = jnp.zeros_like(source)
    residual = source
    local_base = jnp.sum(source * source)
    local_norms = []
    for iteration in range(ITERS):
        scaled = scaled_spectrum(residual, trans_x, trans_r, inv_real, inv_imag)
        if iteration == 0:
            sent = jnp.concatenate([scaled[-1:], coupling[-1:, None]], axis=1)
            got = from_behind(sent, "az", 1)
            from_before = got[:, :2]
            coupling_prev = lax.optimization_barrier(
                jnp.concatenate([got[:, 2], coupling[:-1]], axis=0)
            )
        else:
            from_before = from_behind(scaled[-1:], "az", 1)
        halo_scaled = jnp.concatenate([from_before, from_behind(scaled[:1], "az", -1)], axis=0)
        update = transform(scaled, trans_x, trans_r)
        halo = transform(halo_scaled, trans_x, trans_r, lax.Precision.HIGH)
        before = jnp.concatenate([halo[:1], update[:-1]], axis=0)
        after = jnp.concatenate([update[1:], halo[1:]], axis=0)
        solution = solution + damping * update
        residual = residual - damping * operate(
            update, before, after, coupling, coupling_prev, wavenumber, lateral_x, lateral_r
        )
        local_sum = jnp.sum(residual * residual)
        local_norms.append(local_sum)
    totals = all_sum(jnp.stack([local_base] + local_norms), "az")
    history = jnp.sqrt(totals[1:] / (totals[0] + epsilon))
    return (solution, residual, history)


def solution(mesh):
    return jax.shard_map(
        on_device,
        mesh=mesh,
        in_specs=(P("az", None, None, None), P("az", None, None), P("az", None, None), P(), P()),
        out_specs=(P("az", None, None, None), P("az", None, None, None), P()),
        check_vma=False,
    )
```

```python
import math

import jax
import jax.numpy as jnp
from jax import lax
from jax.sharding import PartitionSpec as P

ITERS = 3


damping = 0.4
epsilon = 1e-06


def from_behind(value, axis, steps):
    count = lax.axis_size(axis)
    pairs = [(source, (source + steps) % count) for source in range(count)]
    return lax.ppermute(value, axis, pairs)


def all_sum(value, axis):
    count = lax.axis_size(axis)
    spread = jnp.broadcast_to(value, (count,) + value.shape)
    gathered = lax.all_to_all(spread, axis, 0, 0, tiled=True)
    total = gathered[0]
    for index in range(1, count):
        total = total + gathered[index]
    return total


def sine_basis(count):
    index = jnp.arange(count).astype(jnp.float32) + 1.0
    angle_grid = math.pi / (count + 1) * index[:, None] * index[None, :]
    table = math.sqrt(2.0 / (count + 1)) * jnp.sin(angle_grid)
    spectrum = 2.0 - 2.0 * jnp.cos(math.pi / (count + 1) * index)
    return (table, spectrum)


def transform(field, trans_x, trans_r, precision=lax.Precision.HIGHEST):
    inner = jnp.einsum("ij,pcjk->pcik", trans_x, field, precision=precision)
    return jnp.einsum("pcik,kl->pcil", inner, trans_r, precision=precision)


def scaled_spectrum(field, trans_x, trans_r, inv_real, inv_imag):
    spectral = transform(field, trans_x, trans_r)
    real_part = spectral[:, 0] * inv_real - spectral[:, 1] * inv_imag
    imag_part = spectral[:, 1] * inv_real + spectral[:, 0] * inv_imag
    return jnp.stack([real_part, imag_part], axis=1)


def lateral(field, lateral_x, lateral_r):
    padded = jnp.pad(field, ((0, 0), (0, 0), (1, 1), (1, 1)))
    stencil = (
        4.0 * field
        - padded[:, :, 2:, 1:-1]
        - padded[:, :, :-2, 1:-1]
        - padded[:, :, 1:-1, 2:]
        - padded[:, :, 1:-1, :-2]
    )
    dense = jnp.einsum("ij,pcjk->pcik", lateral_x, field, precision=lax.Precision.HIGH)
    dense = dense + jnp.einsum("pcik,kl->pcil", field, lateral_r, precision=lax.Precision.HIGH)
    return stencil + dense


def operate(field, before, after, coupling, coupling_prev, wavenumber, lateral_x, lateral_r):
    result = lateral(field, lateral_x, lateral_r) - wavenumber[:, None] * field
    result = (
        result + coupling[:, None] * (field - after) + coupling_prev[:, None] * (field - before)
    )
    return result


def on_device(source, coupling, wavenumber, lateral_x, lateral_r):
    trans_x, spec_x = sine_basis(source.shape[2])
    trans_r, spec_r = sine_basis(source.shape[3])
    denom_real = spec_x[:, None] + spec_r[None, :]
    magnitude = denom_real * denom_real + 1.0
    inv_real = denom_real / magnitude
    inv_imag = -1.0 / magnitude
    trans_x, trans_r, inv_real, inv_imag = lax.optimization_barrier(
        (trans_x, trans_r, inv_real, inv_imag)
    )
    solution = jnp.zeros_like(source)
    residual = source
    local_base = jnp.sum(source * source)
    local_norms = []
    for iteration in range(ITERS):
        scaled = scaled_spectrum(residual, trans_x, trans_r, inv_real, inv_imag)
        if iteration == 0:
            sent = jnp.concatenate([scaled[-1:], coupling[-1:, None]], axis=1)
            got = from_behind(sent, "az", 1)
            from_before = got[:, :2]
            coupling_prev = lax.optimization_barrier(
                jnp.concatenate([got[:, 2], coupling[:-1]], axis=0)
            )
        else:
            from_before = from_behind(scaled[-1:], "az", 1)
        halo_scaled = jnp.concatenate([from_before, from_behind(scaled[:1], "az", -1)], axis=0)
        update = transform(scaled, trans_x, trans_r)
        halo = transform(halo_scaled, trans_x, trans_r, lax.Precision.HIGH)
        extended = lax.optimization_barrier(
            jnp.concatenate([halo[:1], update, halo[1:]], axis=0)
        )
        before = extended[:-2]
        after = extended[2:]
        solution = solution + damping * update
        residual = residual - damping * operate(
            update, before, after, coupling, coupling_prev, wavenumber, lateral_x, lateral_r
        )
        residual = lax.optimization_barrier(residual)
        local_sum = jnp.sum(residual * residual)
        local_norms.append(local_sum)
    totals = all_sum(jnp.stack([local_base] + local_norms), "az")
    history = jnp.sqrt(totals[1:] / (totals[0] + epsilon))
    return (solution, residual, history)


def solution(mesh):
    return jax.shard_map(
        on_device,
        mesh=mesh,
        in_specs=(P("az", None, None, None), P("az", None, None), P("az", None, None), P(), P()),
        out_specs=(P("az", None, None, None), P("az", None, None, None), P()),
        check_vma=False,
    )
```

```python
import math

import jax
import jax.numpy as jnp
from jax import lax
from jax.sharding import PartitionSpec as P

ITERS = 3


damping = 0.4
epsilon = 1e-06


def from_behind(value, axis, steps):
    count = lax.axis_size(axis)
    pairs = [(source, (source + steps) % count) for source in range(count)]
    return lax.ppermute(value, axis, pairs)


def all_sum(value, axis):
    count = lax.axis_size(axis)
    spread = jnp.broadcast_to(value, (count,) + value.shape)
    gathered = lax.all_to_all(spread, axis, 0, 0, tiled=True)
    total = gathered[0]
    for index in range(1, count):
        total = total + gathered[index]
    return total


def sine_basis(count):
    index = jnp.arange(count).astype(jnp.float32) + 1.0
    angle_grid = math.pi / (count + 1) * index[:, None] * index[None, :]
    table = math.sqrt(2.0 / (count + 1)) * jnp.sin(angle_grid)
    spectrum = 2.0 - 2.0 * jnp.cos(math.pi / (count + 1) * index)
    return (table, spectrum)


def transform(field, trans_x, trans_r, precision=lax.Precision.HIGHEST):
    inner = jnp.einsum("ij,pcjk->pcik", trans_x, field, precision=precision)
    return jnp.einsum("pcik,kl->pcil", inner, trans_r, precision=precision)


def scaled_spectrum(field, trans_x, trans_r, inv_real, inv_imag):
    spectral = transform(field, trans_x, trans_r)
    real_part = spectral[:, 0] * inv_real - spectral[:, 1] * inv_imag
    imag_part = spectral[:, 1] * inv_real + spectral[:, 0] * inv_imag
    return jnp.stack([real_part, imag_part], axis=1)


def lateral(field, lateral_x, lateral_r):
    padded = jnp.pad(field, ((0, 0), (0, 0), (1, 1), (1, 1)))
    stencil = (
        4.0 * field
        - padded[:, :, 2:, 1:-1]
        - padded[:, :, :-2, 1:-1]
        - padded[:, :, 1:-1, 2:]
        - padded[:, :, 1:-1, :-2]
    )
    dense = jnp.einsum("ij,pcjk->pcik", lateral_x, field, precision=lax.Precision.HIGH)
    dense = dense + jnp.einsum("pcik,kl->pcil", field, lateral_r, precision=lax.Precision.HIGH)
    return stencil + dense


def operate(field, before, after, coupling, coupling_prev, wavenumber, lateral_x, lateral_r):
    result = lateral(field, lateral_x, lateral_r) - wavenumber[:, None] * field
    result = (
        result + coupling[:, None] * (field - after) + coupling_prev[:, None] * (field - before)
    )
    return result


def on_device(source, coupling, wavenumber, lateral_x, lateral_r):
    trans_x, spec_x = sine_basis(source.shape[2])
    trans_r, spec_r = sine_basis(source.shape[3])
    denom_real = spec_x[:, None] + spec_r[None, :]
    magnitude = denom_real * denom_real + 1.0
    inv_real = denom_real / magnitude
    inv_imag = -1.0 / magnitude
    trans_x, trans_r, inv_real, inv_imag = lax.optimization_barrier(
        (trans_x, trans_r, inv_real, inv_imag)
    )
    solution = jnp.zeros_like(source)
    residual = source
    local_base = jnp.sum(source * source)
    local_norms = []
    for iteration in range(ITERS):
        scaled = lax.optimization_barrier(
            scaled_spectrum(residual, trans_x, trans_r, inv_real, inv_imag)
        )
        if iteration == 0:
            sent = jnp.concatenate([scaled[-1:], coupling[-1:, None]], axis=1)
            got = from_behind(sent, "az", 1)
            from_before = got[:, :2]
            coupling_prev = lax.optimization_barrier(
                jnp.concatenate([got[:, 2], coupling[:-1]], axis=0)
            )
        else:
            from_before = from_behind(scaled[-1:], "az", 1)
        halo_scaled = jnp.concatenate([from_before, from_behind(scaled[:1], "az", -1)], axis=0)
        update = transform(scaled, trans_x, trans_r)
        halo = transform(halo_scaled, trans_x, trans_r, lax.Precision.HIGH)
        extended = lax.optimization_barrier(
            jnp.concatenate([halo[:1], update, halo[1:]], axis=0)
        )
        before = extended[:-2]
        after = extended[2:]
        solution = solution + damping * update
        residual = residual - damping * operate(
            update, before, after, coupling, coupling_prev, wavenumber, lateral_x, lateral_r
        )
        local_sum = jnp.sum(residual * residual)
        local_norms.append(local_sum)
    totals = all_sum(jnp.stack([local_base] + local_norms), "az")
    history = jnp.sqrt(totals[1:] / (totals[0] + epsilon))
    return (solution, residual, history)


def solution(mesh):
    return jax.shard_map(
        on_device,
        mesh=mesh,
        in_specs=(P("az", None, None, None), P("az", None, None), P("az", None, None), P(), P()),
        out_specs=(P("az", None, None, None), P("az", None, None, None), P()),
        check_vma=False,
    )
```

```python
import math

import jax
import jax.numpy as jnp
from jax import lax
from jax.sharding import PartitionSpec as P

ITERS = 3


damping = 0.4
epsilon = 1e-06


def from_behind(value, axis, steps):
    count = lax.axis_size(axis)
    pairs = [(source, (source + steps) % count) for source in range(count)]
    return lax.ppermute(value, axis, pairs)


def all_sum(value, axis):
    count = lax.axis_size(axis)
    spread = jnp.broadcast_to(value, (count,) + value.shape)
    gathered = lax.all_to_all(spread, axis, 0, 0, tiled=True)
    total = gathered[0]
    for index in range(1, count):
        total = total + gathered[index]
    return total


def sine_basis(count):
    index = jnp.arange(count).astype(jnp.float32) + 1.0
    angle_grid = math.pi / (count + 1) * index[:, None] * index[None, :]
    table = math.sqrt(2.0 / (count + 1)) * jnp.sin(angle_grid)
    spectrum = 2.0 - 2.0 * jnp.cos(math.pi / (count + 1) * index)
    return (table, spectrum)


def transform(field, trans_x, trans_r, precision=lax.Precision.HIGHEST):
    inner = jnp.einsum("ij,pcjk->pcik", trans_x, field, precision=precision)
    return jnp.einsum("pcik,kl->pcil", inner, trans_r, precision=precision)


def scaled_spectrum(field, trans_x, trans_r, inv_real, inv_imag):
    spectral = transform(field, trans_x, trans_r)
    real_part = spectral[:, 0] * inv_real - spectral[:, 1] * inv_imag
    imag_part = spectral[:, 1] * inv_real + spectral[:, 0] * inv_imag
    return jnp.stack([real_part, imag_part], axis=1)


def lateral(field, lateral_x, lateral_r):
    padded = jnp.pad(field, ((0, 0), (0, 0), (1, 1), (1, 1)))
    stencil = (
        4.0 * field
        - padded[:, :, 2:, 1:-1]
        - padded[:, :, :-2, 1:-1]
        - padded[:, :, 1:-1, 2:]
        - padded[:, :, 1:-1, :-2]
    )
    dense = jnp.einsum("ij,pcjk->pcik", lateral_x, field, precision=lax.Precision.HIGH)
    dense = dense + jnp.einsum("pcik,kl->pcil", field, lateral_r, precision=lax.Precision.HIGH)
    return stencil + dense


def operate(field, before, after, coupling, coupling_prev, wavenumber, lateral_x, lateral_r):
    result = lateral(field, lateral_x, lateral_r) - wavenumber[:, None] * field
    result = (
        result + coupling[:, None] * (field - after) + coupling_prev[:, None] * (field - before)
    )
    return result


def on_device(source, coupling, wavenumber, lateral_x, lateral_r):
    trans_x, spec_x = sine_basis(source.shape[2])
    trans_r, spec_r = sine_basis(source.shape[3])
    denom_real = spec_x[:, None] + spec_r[None, :]
    magnitude = denom_real * denom_real + 1.0
    inv_real = denom_real / magnitude
    inv_imag = -1.0 / magnitude
    trans_x, trans_r, inv_real, inv_imag = lax.optimization_barrier(
        (trans_x, trans_r, inv_real, inv_imag)
    )
    solution = jnp.zeros_like(source)
    residual = source
    local_base = jnp.sum(source * source)
    local_norms = []
    early = None
    for iteration in range(ITERS):
        if iteration == ITERS - 1:
            early, residual = lax.optimization_barrier(
                (jnp.stack([local_base] + local_norms), residual)
            )
        scaled = scaled_spectrum(residual, trans_x, trans_r, inv_real, inv_imag)
        if iteration == 0:
            sent = jnp.concatenate([scaled[-1:], coupling[-1:, None]], axis=1)
            got = from_behind(sent, "az", 1)
            from_before = got[:, :2]
            coupling_prev = lax.optimization_barrier(
                jnp.concatenate([got[:, 2], coupling[:-1]], axis=0)
            )
        else:
            from_before = from_behind(scaled[-1:], "az", 1)
        halo_scaled = jnp.concatenate([from_before, from_behind(scaled[:1], "az", -1)], axis=0)
        update = transform(scaled, trans_x, trans_r)
        halo = transform(halo_scaled, trans_x, trans_r, lax.Precision.HIGH)
        extended = lax.optimization_barrier(
            jnp.concatenate([halo[:1], update, halo[1:]], axis=0)
        )
        before = extended[:-2]
        after = extended[2:]
        solution = solution + damping * update
        residual = residual - damping * operate(
            update, before, after, coupling, coupling_prev, wavenumber, lateral_x, lateral_r
        )
        local_sum = jnp.sum(residual * residual)
        local_norms.append(local_sum)
    totals = all_sum(jnp.concatenate([early, local_norms[-1][None]]), "az")
    history = jnp.sqrt(totals[1:] / (totals[0] + epsilon))
    return (solution, residual, history)


def solution(mesh):
    return jax.shard_map(
        on_device,
        mesh=mesh,
        in_specs=(P("az", None, None, None), P("az", None, None), P("az", None, None), P(), P()),
        out_specs=(P("az", None, None, None), P("az", None, None, None), P()),
        check_vma=False,
    )
```
